32 devices in a mesh: wide: 8 (over z, y), narrow: 4 (over x, core).
Axes of the slice: x: 2, y: 2, z: 4, core: 2. Of those that a mesh axis runs over, the one named last changes fastest.
Arguments:
- entity_table: bfloat16 [65536, 512], P(('wide', 'narrow')), may hold values from -3 to 3
- relation_table: bfloat16 [4096, 512], replicated, may hold values from -3.59375 to 3.59375
- triple_rel: int32 [8192], P(('wide', 'narrow')), may hold values from 0 to 4095, as said below
- triple_owners: int32 [8192, 2], P(('wide', 'narrow')), may hold values from 0 to 31, all different within a row; in each aligned block of 256 rows (0 to 255, 256 to 511, ...) at most 32 rows name the same one
- triple_local: int32 [8192, 2], P(('wide', 'narrow')), may hold values from 0 to 2047
- negative_ids: int32 [8192], P(('wide', 'narrow')), may hold values from 0 to 2047
Outputs:
- entity_grad: bfloat16 [65536, 512], P(('wide', 'narrow'))
- relation_grad: bfloat16 [4096, 512], replicated
- loss: float32 [8192], P(('wide', 'narrow'))
The draws below stay inside these ranges and needn't reach their ends.
Inputs may be any that keep to these rules, and one draw needn't show every extreme that they name: `triple_owners`: the two owners of a triple differ. Among the triples of one device no owner is named more than 32 times, and in every draw the triples of some device name some owner exactly 32 times. `triple_rel`: relation group k holds relations k * 128 to (k + 1) * 128 - 1. Among the triples of each device the relations of exactly one group appear exactly 16 times, and those of every other group appear equally often up to one, at most 16 times.
All inputs are finite; a program needn't handle non-finite values.
Results may differ from the reference program's by a relative error of at most 0.0075.
Values may be sent and summed in bfloat16 or wider, within the bound.
No kernel may reach another device: no remote copies, remote signals or barrier semaphores. Data moves between devices by JAX's collectives and lax.ppermute only.
A program may use at most 128 MiB of HBM per device.

```python
import math
import jax
import jax.numpy as jnp
import numpy as np
from jax import lax

EMB = 256
NREL = 4096
ENT_DEV = 2048
TRI_DEV = 256
NEG_DEV = 256
CAP = 32
REL_DEV = 128
RCAP = 16
ENTITIES = 65536
TRIPLES = 8192
NEG_ALL = 8192
GROUP_NEG = 1024
N_WIDE = 8
N_NARROW = 4
DEVICES = 32


def draw_triple_rel(key, part):
    base = jax.random.fold_in(key, 11)
    key_hot, key_within, key_order = jax.random.split(base, 3)
    hot_group = jax.random.randint(key_hot, (DEVICES,), 0, DEVICES)
    position = jnp.arange(TRI_DEV, dtype=jnp.int32)
    spread = jnp.mod(position - RCAP, DEVICES - 1)
    offsets = jnp.where(position < RCAP, 0, 1 + spread).astype(jnp.int32)
    group = jnp.mod(hot_group[:, None] + offsets[None, :], DEVICES)
    within = jax.random.randint(key_within, (DEVICES, TRI_DEV), 0, REL_DEV)
    relation = group * REL_DEV + within
    order_keys = jax.random.split(key_order, DEVICES)
    orders = jax.vmap(lambda single: jax.random.permutation(single, TRI_DEV))(order_keys)
    relation = jnp.take_along_axis(relation, orders, axis=1)
    return relation.reshape(-1).astype(jnp.int32)


def touch_ends(entries, rng, least, top_value):
    dims = entries.shape
    spot = [jax.random.randint(jax.random.fold_in(rng, axis), (), 0, dims[axis]) for axis in range(len(dims))]
    entries = entries.at[tuple(spot)].set(least)
    longest = dims.index(max(dims))
    spot[longest] = (spot[longest] + 1) % dims[longest]
    return entries.at[tuple(spot)].set(top_value)


def levels(own_key, extent, cuts, smallest, top_value):
    def one(axis_at, blocks):
        heights = jax.random.uniform(jax.random.fold_in(jax.random.fold_in(own_key, 6), axis_at), (blocks,), jnp.float32, smallest / len(cuts), top_value / len(cuts))
        return jnp.repeat(jnp.exp(heights), extent[axis_at] // blocks).reshape((-1,) + (1,) * (len(extent) - axis_at - 1))

    factor_of = one(*cuts[0])
    for cut in cuts[1:]:
        factor_of = factor_of * one(*cut)
    return factor_of


def deal_out(rng, own, number, rows, amount, top, most, lean):
    ranking = jax.random.permutation(rng, amount)
    heavy_load, ordinary = shares(amount, rows * top, most, lean, True), shares(amount, rows * top, most, lean, False)
    places = jnp.arange(amount)

    def named(lengths, rotation):
        used = int((lengths > 0).sum())
        fixed = max(1, used // 4)
        shifted = fixed + (places - fixed + rotation * (used - fixed)) % max(1, amount - fixed)
        return jnp.zeros((amount,), jnp.int32).at[ranking[jnp.where(places < fixed, places, shifted)]].set(jnp.asarray(lengths, jnp.int32))

    lengths = jnp.where(number % 4 == 0, named(heavy_load, number // 4), named(ordinary, number - number // 4 - 1))
    mixed = jax.random.permutation(jax.random.fold_in(own, 3), amount)
    giver, taker = mixed[0:amount // 2 * 2:2], mixed[1:amount // 2 * 2:2]
    margin = jnp.minimum(lengths[giver] - 1, most - lengths[taker]) // 2
    margin = jnp.where((giver == ranking[0]) | (taker == ranking[0]) | (lengths[taker] == 0), 0, jnp.maximum(margin, 0))
    shifted = jax.random.randint(jax.random.fold_in(own, 4), (amount // 2,), 0, 1 << 20) % (margin + 1)
    lengths = lengths.at[giver].add(-shifted).at[taker].add(shifted)
    members = jnp.searchsorted(jnp.cumsum(lengths), jnp.arange(rows * top), side="right").astype(jnp.int32)
    grid = members.reshape(top, rows).T
    grid = grid[jax.random.permutation(jax.random.fold_in(own, 1), rows)]
    rotation = jax.random.randint(jax.random.fold_in(own, 2), (rows, 1), 0, top)
    return jnp.take_along_axis(grid, (jnp.arange(top)[None, :] + rotation) % top, axis=1)


def shares(count, total, limit, lean, full):
    loads = [(1 << 20) // math.isqrt(grade ** lean) + 1 for grade in range(1, count + 1)]
    largest = limit if full else min(limit, max(-(-total // count), total * loads[0] // sum(loads)))
    least = 1 if total - largest >= count - 1 else 0
    counts, rest = [largest] + [least] * (count - 1), total - largest - least * (count - 1)
    while rest > 0:
        candidates = [i for i in range(1, count) if counts[i] < largest] or [i for i in range(1, count) if counts[i] < limit]
        pool, remaining = sum([loads[i] for i in candidates]), rest
        for i in candidates:
            more = min(limit - counts[i], max(1, remaining * loads[i] // pool), rest)
            counts[i] = counts[i] + more
            rest = rest - more
    return np.array(counts)


def bell_draw(stream_key, extent, scale, bound, cuts=(), held_as=jnp.bfloat16):
    drawn = jax.random.normal(stream_key, extent, jnp.float32) * scale
    if len(cuts) > 0:
        drawn = levels(stream_key, extent, cuts, -0.22, 0.18) * drawn
    return jnp.clip(drawn, min=-bound, max=bound).astype(held_as)


def setup_inputs(seed: int = 0) -> dict:
    splits = jax.random.split(jax.random.key(seed), 7)
    entity_table = bell_draw(splits[0], (ENTITIES, 2 * EMB), 0.5, 3.0, ((0, 32),))
    relation_table = bell_draw(splits[1], (NREL, 2 * EMB), 0.6, 3.59375)
    triple_rel = draw_triple_rel(jax.random.fold_in(splits[6], 71), 0)
    triple_owners_keys = jax.random.split(jax.random.fold_in(splits[3], 1), TRIPLES // TRI_DEV)
    triple_owners_turns = jax.random.permutation(jax.random.fold_in(splits[3], 3), TRIPLES // TRI_DEV)
    triple_owners = jax.vmap(lambda own, number: deal_out(jax.random.fold_in(splits[3], 2), own, number, TRI_DEV, DEVICES, 2, CAP, 2))(triple_owners_keys, triple_owners_turns).reshape((TRIPLES, 2))
    triple_local = touch_ends(jax.random.randint(splits[4], (TRIPLES, 2), 0, ENT_DEV), jax.random.fold_in(splits[4], 1), 0, ENT_DEV - 1).astype(jnp.int32)
    negative_ids = touch_ends(jax.random.randint(splits[5], (NEG_ALL,), 0, ENT_DEV), jax.random.fold_in(splits[5], 1), 0, ENT_DEV - 1).astype(jnp.int32)
    return {"entity_table": entity_table, "relation_table": relation_table, "triple_rel": triple_rel, "triple_owners": triple_owners, "triple_local": triple_local, "negative_ids": negative_ids}


def swap_halves(rows):
    half_width = rows.shape[-1] // 2
    return jnp.concatenate([rows[..., half_width:], rows[..., :half_width]], axis=-1)


def reference(entity_table, relation_table, triple_rel, triple_owners, triple_local, negative_ids):
    global_rows = (triple_owners * ENT_DEV + triple_local).astype(jnp.int32)
    head_rows = jnp.take(entity_table, global_rows[:, 0], axis=0)
    tail_rows = jnp.take(entity_table, global_rows[:, 1], axis=0)
    rel_rows = jnp.take(relation_table, triple_rel, axis=0)
    query = (0.5 * swap_halves(head_rows).astype(jnp.float32) * swap_halves(rel_rows).astype(jnp.float32)).astype(jnp.bfloat16)
    positive = jnp.sum(query.astype(jnp.float32) * tail_rows.astype(jnp.float32), axis=1)
    holder = (jnp.arange(NEG_ALL, dtype=jnp.int32) // NEG_DEV).astype(jnp.int32)
    neg_global = (holder * ENT_DEV + negative_ids).astype(jnp.int32)
    neg_rows = jnp.take(entity_table, neg_global, axis=0)
    group_rows = TRI_DEV * N_NARROW
    grouped_query = query.reshape(N_WIDE, group_rows, 2 * EMB)
    grouped_negs = neg_rows.reshape(N_WIDE, GROUP_NEG, 2 * EMB)

    def per_group(pair):
        queries, group_negs = pair
        scores = jnp.dot(queries, group_negs.T, preferred_element_type=jnp.float32)
        soft_sum = jnp.sum(jax.nn.softplus(scores), axis=1)
        weights = (jax.nn.sigmoid(scores) / GROUP_NEG).astype(jnp.bfloat16)
        neg_term = jnp.dot(weights, group_negs, preferred_element_type=jnp.float32)
        group_grad = jnp.dot(weights.T, queries, preferred_element_type=jnp.float32)
        return soft_sum, neg_term, group_grad

    soft_sum, neg_term, neg_grad = lax.map(per_group, (grouped_query, grouped_negs))
    soft_sum = soft_sum.reshape(TRIPLES)
    neg_term = neg_term.reshape(TRIPLES, 2 * EMB)
    neg_grad = neg_grad.reshape(NEG_ALL, 2 * EMB)
    loss = jax.nn.softplus(-positive) + soft_sum / GROUP_NEG
    pos_weight = -jax.nn.sigmoid(-positive)
    query_grad = pos_weight[:, None] * tail_rows.astype(jnp.float32) + neg_term
    tail_grad = pos_weight[:, None] * query.astype(jnp.float32)
    head_grad = 0.5 * swap_halves(query_grad) * rel_rows.astype(jnp.float32)
    rel_part = 0.5 * swap_halves(query_grad) * head_rows.astype(jnp.float32)
    entity_grad = jnp.zeros((ENTITIES, 2 * EMB), jnp.float32)
    entity_grad = entity_grad.at[global_rows[:, 0]].add(head_grad)
    entity_grad = entity_grad.at[global_rows[:, 1]].add(tail_grad)
    entity_grad = entity_grad.at[neg_global].add(neg_grad)
    relation_grad = jax.ops.segment_sum(rel_part, triple_rel, num_segments=NREL)
    return entity_grad.astype(jnp.bfloat16), relation_grad.astype(jnp.bfloat16), loss
```

```python
import jax
import jax.numpy as jnp
from jax import lax
from jax.sharding import PartitionSpec as P

AXES = ("wide", "narrow")


def swap_halves(rows):
    half_width = rows.shape[-1] // 2
    return jnp.concatenate([rows[..., half_width:], rows[..., :half_width]], axis=-1)


def slot_ranks(targets, count):
    onehot = (targets[:, None] == jnp.arange(count, dtype=jnp.int32)[None, :]).astype(jnp.int32)
    return jnp.sum((jnp.cumsum(onehot, axis=0) - onehot) * onehot, axis=1)


def split_dot(spec, onehot, values, parts=2):
    total = None
    rest = values
    for _ in range(parts):
        piece = rest.astype(jnp.bfloat16)
        rest = rest - piece.astype(jnp.float32)
        term = jnp.einsum(spec, onehot, piece, preferred_element_type=jnp.float32)
        total = term if total is None else total + term
    return total


def body(entity_table, relation_table, triple_rel, triple_owners, triple_local, negative_ids):
    wide_count = lax.axis_size("wide")
    narrow_count = lax.axis_size("narrow")
    device_count = wide_count * narrow_count
    triples = triple_rel.shape[0]
    row_width = entity_table.shape[1]
    entity_rows = entity_table.shape[0]
    capacity = max(2, 4 * triples // device_count)
    rel_capacity = max(1, 2 * triples // device_count)
    rel_per_group = relation_table.shape[0] // device_count

    owners = triple_owners.reshape(-1)
    local_rows = triple_local.reshape(-1)
    ent_pos = owners * capacity + slot_ranks(owners, device_count)
    rel_group = triple_rel // rel_per_group
    rel_pos = rel_group * rel_capacity + slot_ranks(rel_group, device_count)
    rel_local = triple_rel - rel_group * rel_per_group

    ent_place = jnp.arange(device_count * capacity, dtype=jnp.int32)[:, None] == ent_pos[None, :]
    rel_place = jnp.arange(device_count * rel_capacity, dtype=jnp.int32)[:, None] == rel_pos[None, :]
    send_ent_ids = jnp.sum(jnp.where(ent_place, local_rows[None, :], 0), axis=1)
    send_rel_ids = jnp.sum(jnp.where(rel_place, rel_local[None, :], 0), axis=1)
    send_ids = jnp.concatenate(
        [
            send_ent_ids.reshape(device_count, capacity),
            send_rel_ids.reshape(device_count, rel_capacity),
        ],
        axis=1,
    )
    recv_ids = lax.all_to_all(send_ids, AXES, split_axis=0, concat_axis=0, tiled=True)
    asked_ids = recv_ids[:, :capacity].reshape(-1)
    rel_ids_in = recv_ids[:, capacity:].reshape(-1)

    served = jnp.take(entity_table, asked_ids, axis=0).reshape(device_count, capacity, row_width)
    got_rows = lax.all_to_all(served, AXES, split_axis=0, concat_axis=0, tiled=True)
    got_rows = got_rows.reshape(device_count * capacity, row_width)
    ent_place_bf = ent_place.astype(jnp.bfloat16)
    fetched = jnp.einsum(
        "sj,sc->jc", ent_place_bf, got_rows, preferred_element_type=jnp.float32
    ).astype(jnp.bfloat16)
    fetched = fetched.reshape(triples, 2, row_width)
    head_rows = fetched[:, 0]
    tail_rows = fetched[:, 1]
    rel_rows = jnp.take(relation_table, triple_rel, axis=0)
    query = (
        0.5 * swap_halves(head_rows).astype(jnp.float32) * swap_halves(rel_rows).astype(jnp.float32)
    ).astype(jnp.bfloat16)
    positive = jnp.sum(query.astype(jnp.float32) * tail_rows.astype(jnp.float32), axis=1)

    own_negs = jnp.take(entity_table, negative_ids, axis=0)
    gathered = lax.all_gather(own_negs, "narrow", axis=0, tiled=True)
    group_neg = gathered.shape[0]
    scores = jnp.einsum("tc,kc->tk", query, gathered, preferred_element_type=jnp.float32)
    loss = jax.nn.softplus(-positive) + jnp.sum(jax.nn.softplus(scores), axis=1) / group_neg
    neg_weights = (jax.nn.sigmoid(scores) / group_neg).astype(jnp.bfloat16)
    pos_weight = -jax.nn.sigmoid(-positive)
    query_grad = pos_weight[:, None] * tail_rows.astype(jnp.float32) + jnp.dot(
        neg_weights, gathered, preferred_element_type=jnp.float32
    )
    tail_grad = pos_weight[:, None] * query.astype(jnp.float32)
    head_grad = 0.5 * swap_halves(query_grad) * rel_rows.astype(jnp.float32)
    rel_part = 0.5 * swap_halves(query_grad) * head_rows.astype(jnp.float32)

    group_query = lax.all_gather(query, "narrow", axis=0, tiled=True)
    own_scores = jnp.einsum("tc,kc->tk", group_query, own_negs, preferred_element_type=jnp.float32)
    own_weights = (jax.nn.sigmoid(own_scores) / group_neg).astype(jnp.bfloat16)
    neg_grad = jnp.einsum("tk,tc->kc", own_weights, group_query, preferred_element_type=jnp.float32)

    ent_grads = jnp.stack([head_grad, tail_grad], axis=1).reshape(2 * triples, row_width)
    send_ent = split_dot("sj,jc->sc", ent_place_bf, ent_grads, parts=3)
    send_rel = split_dot("sj,jc->sc", rel_place.astype(jnp.bfloat16), rel_part, parts=3)
    send_grads = jnp.concatenate(
        [
            send_ent.reshape(device_count, capacity, row_width),
            send_rel.reshape(device_count, rel_capacity, row_width),
        ],
        axis=1,
    )
    back_grads = lax.all_to_all(send_grads, AXES, split_axis=0, concat_axis=0, tiled=True)
    back_ent = back_grads[:, :capacity].reshape(-1, row_width)
    back_rel = back_grads[:, capacity:].reshape(-1, row_width)

    ids_all = jnp.concatenate([asked_ids, negative_ids])
    grads_all = jnp.concatenate([back_ent, neg_grad], axis=0)
    ent_onehot = (
        ids_all[:, None] == jnp.arange(entity_rows, dtype=jnp.int32)[None, :]
    ).astype(jnp.bfloat16)
    entity_grad = split_dot("se,sc->ec", ent_onehot, grads_all)

    rel_onehot = (
        rel_ids_in[:, None] == jnp.arange(rel_per_group, dtype=jnp.int32)[None, :]
    ).astype(jnp.bfloat16)
    own_rel_grad = split_dot("sr,sc->rc", rel_onehot, back_rel).astype(jnp.bfloat16)
    relation_grad = lax.all_gather(own_rel_grad, AXES, axis=0, tiled=True)
    return (entity_grad.astype(jnp.bfloat16), relation_grad, loss)


def solution(mesh):
    return jax.shard_map(
        body,
        mesh=mesh,
        in_specs=(
            P(AXES, None),
            P(),
            P(AXES),
            P(AXES, None),
            P(AXES, None),
            P(AXES),
        ),
        out_specs=(P(AXES, None), P(), P(AXES)),
        check_vma=False,
    )
```

```python
import jax
import jax.numpy as jnp
from jax import lax
from jax.sharding import PartitionSpec as P

AXES = ("wide", "narrow")


def swap_halves(rows):
    half_width = rows.shape[-1] // 2
    return jnp.concatenate([rows[..., half_width:], rows[..., :half_width]], axis=-1)


def slot_ranks(targets, count):
    onehot = (targets[:, None] == jnp.arange(count, dtype=jnp.int32)[None, :]).astype(jnp.int32)
    return jnp.sum((jnp.cumsum(onehot, axis=0) - onehot) * onehot, axis=1)


def split_dot(spec, onehot, values, parts=2):
    total = None
    rest = values
    for _ in range(parts):
        piece = rest.astype(jnp.bfloat16)
        rest = rest - piece.astype(jnp.float32)
        term = jnp.einsum(spec, onehot, piece, preferred_element_type=jnp.float32)
        total = term if total is None else total + term
    return total


def body(entity_table, relation_table, triple_rel, triple_owners, triple_local, negative_ids):
    wide_count = lax.axis_size("wide")
    narrow_count = lax.axis_size("narrow")
    device_count = wide_count * narrow_count
    triples = triple_rel.shape[0]
    row_width = entity_table.shape[1]
    entity_rows = entity_table.shape[0]
    capacity = max(2, 4 * triples // device_count)
    rel_capacity = max(1, 2 * triples // device_count)
    rel_per_group = relation_table.shape[0] // device_count

    owners = triple_owners.reshape(-1)
    local_rows = triple_local.reshape(-1)
    ent_pos = owners * capacity + slot_ranks(owners, device_count)
    rel_group = triple_rel // rel_per_group
    rel_owner = (rel_group % wide_count) * narrow_count + rel_group // wide_count
    rel_pos = rel_owner * rel_capacity + slot_ranks(rel_owner, device_count)
    rel_local = triple_rel - rel_group * rel_per_group

    ent_place = jnp.arange(device_count * capacity, dtype=jnp.int32)[:, None] == ent_pos[None, :]
    rel_place = jnp.arange(device_count * rel_capacity, dtype=jnp.int32)[:, None] == rel_pos[None, :]
    send_ent_ids = jnp.sum(jnp.where(ent_place, local_rows[None, :], 0), axis=1)
    send_rel_ids = jnp.sum(jnp.where(rel_place, rel_local[None, :], 0), axis=1)
    send_ids = jnp.concatenate(
        [
            send_ent_ids.reshape(device_count, capacity),
            send_rel_ids.reshape(device_count, rel_capacity),
        ],
        axis=1,
    )
    recv_ids = lax.all_to_all(send_ids, AXES, split_axis=0, concat_axis=0, tiled=True)
    asked_ids = recv_ids[:, :capacity].reshape(-1)
    rel_ids_in = recv_ids[:, capacity:].reshape(-1)

    served = jnp.take(entity_table, asked_ids, axis=0).reshape(device_count, capacity, row_width)
    got_rows = lax.all_to_all(served, AXES, split_axis=0, concat_axis=0, tiled=True)
    got_rows = got_rows.reshape(device_count * capacity, row_width)
    ent_place_bf = ent_place.astype(jnp.bfloat16)
    fetched = jnp.einsum(
        "sj,sc->jc", ent_place_bf, got_rows, preferred_element_type=jnp.float32
    ).astype(jnp.bfloat16)
    fetched = fetched.reshape(triples, 2, row_width)
    head_rows = fetched[:, 0]
    tail_rows = fetched[:, 1]
    rel_rows = jnp.take(relation_table, triple_rel, axis=0)
    query = (
        0.5 * swap_halves(head_rows).astype(jnp.float32) * swap_halves(rel_rows).astype(jnp.float32)
    ).astype(jnp.bfloat16)
    positive = jnp.sum(query.astype(jnp.float32) * tail_rows.astype(jnp.float32), axis=1)

    own_negs = jnp.take(entity_table, negative_ids, axis=0)
    gathered = lax.all_gather(own_negs, "narrow", axis=0, tiled=True)
    group_neg = gathered.shape[0]
    scores = jnp.einsum("tc,kc->tk", query, gathered, preferred_element_type=jnp.float32)
    loss = jax.nn.softplus(-positive) + jnp.sum(jax.nn.softplus(scores), axis=1) / group_neg
    neg_weights = (jax.nn.sigmoid(scores) / group_neg).astype(jnp.bfloat16)
    pos_weight = -jax.nn.sigmoid(-positive)
    query_grad = pos_weight[:, None] * tail_rows.astype(jnp.float32) + jnp.dot(
        neg_weights, gathered, preferred_element_type=jnp.float32
    )
    tail_grad = pos_weight[:, None] * query.astype(jnp.float32)
    head_grad = 0.5 * swap_halves(query_grad) * rel_rows.astype(jnp.float32)
    rel_part = 0.5 * swap_halves(query_grad) * head_rows.astype(jnp.float32)

    group_query = lax.all_gather(query, "narrow", axis=0, tiled=True)
    own_scores = jnp.einsum("tc,kc->tk", group_query, own_negs, preferred_element_type=jnp.float32)
    own_weights = (jax.nn.sigmoid(own_scores) / group_neg).astype(jnp.bfloat16)
    neg_grad = jnp.einsum("tk,tc->kc", own_weights, group_query, preferred_element_type=jnp.float32)

    ent_grads = jnp.stack([head_grad, tail_grad], axis=1).reshape(2 * triples, row_width)
    send_ent = jnp.einsum(
        "sj,jc->sc", ent_place_bf, ent_grads.astype(jnp.bfloat16), preferred_element_type=jnp.float32
    ).astype(jnp.bfloat16)
    send_rel = jnp.einsum(
        "sj,jc->sc",
        rel_place.astype(jnp.bfloat16),
        rel_part.astype(jnp.bfloat16),
        preferred_element_type=jnp.float32,
    ).astype(jnp.bfloat16)
    send_grads = jnp.concatenate(
        [
            send_ent.reshape(device_count, capacity, row_width),
            send_rel.reshape(device_count, rel_capacity, row_width),
        ],
        axis=1,
    )
    back_grads = lax.all_to_all(send_grads, AXES, split_axis=0, concat_axis=0, tiled=True)
    back_ent = back_grads[:, :capacity].reshape(-1, row_width)
    back_rel = back_grads[:, capacity:].reshape(-1, row_width)

    entity_iota = jnp.arange(entity_rows, dtype=jnp.int32)[None, :]
    asked_onehot = (asked_ids[:, None] == entity_iota).astype(jnp.bfloat16)
    neg_onehot = (negative_ids[:, None] == entity_iota).astype(jnp.bfloat16)
    entity_grad = jnp.einsum(
        "se,sc->ec", asked_onehot, back_ent, preferred_element_type=jnp.float32
    ) + split_dot("se,sc->ec", neg_onehot, neg_grad)

    rel_onehot = (
        rel_ids_in[:, None] == jnp.arange(rel_per_group, dtype=jnp.int32)[None, :]
    ).astype(jnp.bfloat16)
    own_rel_grad = jnp.einsum(
        "sr,sc->rc", rel_onehot, back_rel, preferred_element_type=jnp.float32
    ).astype(jnp.bfloat16)
    relation_grad = lax.all_gather(own_rel_grad, "wide", axis=0, tiled=True)
    relation_grad = lax.all_gather(relation_grad, "narrow", axis=0, tiled=True)
    return (entity_grad.astype(jnp.bfloat16), relation_grad, loss)


def solution(mesh):
    return jax.shard_map(
        body,
        mesh=mesh,
        in_specs=(
            P(AXES, None),
            P(),
            P(AXES),
            P(AXES, None),
            P(AXES, None),
            P(AXES),
        ),
        out_specs=(P(AXES, None), P(), P(AXES)),
        check_vma=False,
    )
```

```python
import jax
import jax.numpy as jnp
from jax import lax
from jax.sharding import PartitionSpec as P

AXES = ("wide", "narrow")


def swap_halves(rows):
    half_width = rows.shape[-1] // 2
    return jnp.concatenate([rows[..., half_width:], rows[..., :half_width]], axis=-1)


def slot_ranks(targets, count):
    onehot = (targets[:, None] == jnp.arange(count, dtype=jnp.int32)[None, :]).astype(jnp.int32)
    return jnp.sum((jnp.cumsum(onehot, axis=0) - onehot) * onehot, axis=1)


def body(entity_table, relation_table, triple_rel, triple_owners, triple_local, negative_ids):
    wide_count = lax.axis_size("wide")
    narrow_count = lax.axis_size("narrow")
    device_count = wide_count * narrow_count
    triples = triple_rel.shape[0]
    row_width = entity_table.shape[1]
    entity_rows = entity_table.shape[0]
    capacity = max(2, 4 * triples // device_count)
    rel_capacity = max(1, 2 * triples // device_count)
    rel_per_group = relation_table.shape[0] // device_count

    owners = triple_owners.reshape(-1)
    local_rows = triple_local.reshape(-1)
    ent_pos = owners * capacity + slot_ranks(owners, device_count)
    rel_group = triple_rel // rel_per_group
    rel_owner = (rel_group % wide_count) * narrow_count + rel_group // wide_count
    rel_pos = rel_owner * rel_capacity + slot_ranks(rel_owner, device_count)
    rel_local = triple_rel - rel_group * rel_per_group

    ent_place = jnp.arange(device_count * capacity, dtype=jnp.int32)[:, None] == ent_pos[None, :]
    rel_place = jnp.arange(device_count * rel_capacity, dtype=jnp.int32)[:, None] == rel_pos[None, :]
    send_ent_ids = jnp.sum(jnp.where(ent_place, local_rows[None, :], 0), axis=1)
    send_rel_ids = jnp.sum(jnp.where(rel_place, rel_local[None, :], 0), axis=1)
    send_ids = jnp.concatenate(
        [
            send_ent_ids.reshape(device_count, capacity),
            send_rel_ids.reshape(device_count, rel_capacity),
        ],
        axis=1,
    )
    recv_ids = lax.all_to_all(send_ids, AXES, split_axis=0, concat_axis=0, tiled=True)
    asked_ids = recv_ids[:, :capacity].reshape(-1)
    rel_ids_in = recv_ids[:, capacity:].reshape(-1)

    served = jnp.take(entity_table, asked_ids, axis=0).reshape(device_count, capacity, row_width)
    got_rows = lax.all_to_all(served, AXES, split_axis=0, concat_axis=0, tiled=True)
    got_rows = got_rows.reshape(device_count * capacity, row_width)
    ent_place_bf = ent_place.astype(jnp.bfloat16)
    fetched = jnp.einsum(
        "sj,sc->jc", ent_place_bf, got_rows, preferred_element_type=jnp.float32
    ).astype(jnp.bfloat16)
    fetched = fetched.reshape(triples, 2, row_width)
    head_rows = fetched[:, 0]
    tail_rows = fetched[:, 1]
    rel_rows = jnp.take(relation_table, triple_rel, axis=0)
    query = (
        0.5 * swap_halves(head_rows).astype(jnp.float32) * swap_halves(rel_rows).astype(jnp.float32)
    ).astype(jnp.bfloat16)
    positive = jnp.sum(query.astype(jnp.float32) * tail_rows.astype(jnp.float32), axis=1)

    own_negs = jnp.take(entity_table, negative_ids, axis=0)
    gathered = lax.all_gather(own_negs, "narrow", axis=0, tiled=True)
    group_neg = gathered.shape[0]
    scores = jnp.einsum("tc,kc->tk", query, gathered, preferred_element_type=jnp.float32)
    loss = jax.nn.softplus(-positive) + jnp.sum(jax.nn.softplus(scores), axis=1) / group_neg
    neg_weights = (jax.nn.sigmoid(scores) / group_neg).astype(jnp.bfloat16)
    pos_weight = -jax.nn.sigmoid(-positive)
    query_grad = pos_weight[:, None] * tail_rows.astype(jnp.float32) + jnp.dot(
        neg_weights, gathered, preferred_element_type=jnp.float32
    )
    tail_grad = pos_weight[:, None] * query.astype(jnp.float32)
    head_grad = 0.5 * swap_halves(query_grad) * rel_rows.astype(jnp.float32)
    rel_part = 0.5 * swap_halves(query_grad) * head_rows.astype(jnp.float32)

    group_query = lax.all_gather(query, "narrow", axis=0, tiled=True)
    group_query, head_grad, tail_grad, rel_part = lax.optimization_barrier(
        (group_query, head_grad, tail_grad, rel_part)
    )

    send_rel = jnp.einsum(
        "sj,jc->sc",
        rel_place.astype(jnp.bfloat16),
        rel_part.astype(jnp.bfloat16),
        preferred_element_type=jnp.float32,
    ).astype(jnp.bfloat16)
    back_rel = lax.all_to_all(
        send_rel.reshape(device_count, rel_capacity, row_width), AXES, split_axis=0, concat_axis=0, tiled=True
    ).reshape(-1, row_width)
    rel_onehot = (
        rel_ids_in[:, None] == jnp.arange(rel_per_group, dtype=jnp.int32)[None, :]
    ).astype(jnp.bfloat16)
    own_rel_grad = jnp.einsum(
        "sr,sc->rc", rel_onehot, back_rel, preferred_element_type=jnp.float32
    ).astype(jnp.bfloat16)

    ent_grads = jnp.stack([head_grad, tail_grad], axis=1).reshape(2 * triples, row_width)
    send_ent = jnp.einsum(
        "sj,jc->sc", ent_place_bf, ent_grads.astype(jnp.bfloat16), preferred_element_type=jnp.float32
    ).astype(jnp.bfloat16)
    own_rel_grad, send_ent = lax.optimization_barrier((own_rel_grad, send_ent))
    relation_grad = lax.all_gather(own_rel_grad, "wide", axis=0, tiled=True)
    relation_grad = lax.all_gather(relation_grad, "narrow", axis=0, tiled=True)
    back_ent = lax.all_to_all(
        send_ent.reshape(device_count, capacity, row_width), AXES, split_axis=0, concat_axis=0, tiled=True
    ).reshape(-1, row_width)

    own_scores = jnp.einsum("tc,kc->tk", group_query, own_negs, preferred_element_type=jnp.float32)
    own_weights = (jax.nn.sigmoid(own_scores) / group_neg).astype(jnp.bfloat16)
    neg_grad = jnp.einsum("tk,tc->kc", own_weights, group_query, preferred_element_type=jnp.float32)

    entity_iota = jnp.arange(entity_rows, dtype=jnp.int32)[None, :]
    asked_onehot = (asked_ids[:, None] == entity_iota).astype(jnp.bfloat16)
    neg_onehot = (negative_ids[:, None] == entity_iota).astype(jnp.bfloat16)
    entity_grad = jnp.einsum(
        "se,sc->ec", asked_onehot, back_ent, preferred_element_type=jnp.float32
    ) + jnp.einsum(
        "se,sc->ec", neg_onehot, neg_grad.astype(jnp.bfloat16), preferred_element_type=jnp.float32
    )
    return (entity_grad.astype(jnp.bfloat16), relation_grad, loss)


def solution(mesh):
    return jax.shard_map(
        body,
        mesh=mesh,
        in_specs=(
            P(AXES, None),
            P(),
            P(AXES),
            P(AXES, None),
            P(AXES, None),
            P(AXES),
        ),
        out_specs=(P(AXES, None), P(), P(AXES)),
        check_vma=False,
    )
```

```python
import jax
import jax.numpy as jnp
from jax import lax
from jax.sharding import PartitionSpec as P

AXES = ("wide", "narrow")


def swap_halves(rows):
    half_width = rows.shape[-1] // 2
    return jnp.concatenate([rows[..., half_width:], rows[..., :half_width]], axis=-1)


def slot_ranks(targets, count):
    onehot = (targets[:, None] == jnp.arange(count, dtype=jnp.int32)[None, :]).astype(jnp.int32)
    return jnp.sum((jnp.cumsum(onehot, axis=0) - onehot) * onehot, axis=1)


def body(entity_table, relation_table, triple_rel, triple_owners, triple_local, negative_ids):
    wide_count = lax.axis_size("wide")
    narrow_count = lax.axis_size("narrow")
    device_count = wide_count * narrow_count
    triples = triple_rel.shape[0]
    row_width = entity_table.shape[1]
    entity_rows = entity_table.shape[0]
    capacity = max(2, 4 * triples // device_count)
    rel_capacity = max(1, 2 * triples // device_count)
    rel_per_group = relation_table.shape[0] // device_count

    owners = triple_owners.reshape(-1)
    local_rows = triple_local.reshape(-1)
    ent_pos = owners * capacity + slot_ranks(owners, device_count)
    rel_group = triple_rel // rel_per_group
    rel_pos = rel_group * rel_capacity + slot_ranks(rel_group, device_count)
    rel_local = triple_rel - rel_group * rel_per_group

    ent_place = jnp.arange(device_count * capacity, dtype=jnp.int32)[:, None] == ent_pos[None, :]
    rel_place = jnp.arange(device_count * rel_capacity, dtype=jnp.int32)[:, None] == rel_pos[None, :]
    send_ent_ids = jnp.sum(jnp.where(ent_place, local_rows[None, :], 0), axis=1)
    send_rel_ids = jnp.sum(jnp.where(rel_place, rel_local[None, :], 0), axis=1)
    send_ids = jnp.concatenate(
        [
            send_ent_ids.reshape(device_count, capacity),
            send_rel_ids.reshape(device_count, rel_capacity),
        ],
        axis=1,
    )
    recv_ids = lax.all_to_all(send_ids, AXES, split_axis=0, concat_axis=0, tiled=True)
    asked_ids = recv_ids[:, :capacity].reshape(-1)
    rel_ids_in = recv_ids[:, capacity:].reshape(-1)

    served = jnp.take(entity_table, asked_ids, axis=0).reshape(device_count, capacity, row_width)
    got_rows = lax.all_to_all(served, AXES, split_axis=0, concat_axis=0, tiled=True)
    got_rows = got_rows.reshape(device_count * capacity, row_width)
    ent_place_bf = ent_place.astype(jnp.bfloat16)
    fetched = jnp.einsum(
        "sj,sc->jc", ent_place_bf, got_rows, preferred_element_type=jnp.float32
    ).astype(jnp.bfloat16)
    fetched = fetched.reshape(triples, 2, row_width)
    head_rows = fetched[:, 0]
    tail_rows = fetched[:, 1]
    rel_rows = jnp.take(relation_table, triple_rel, axis=0)
    query = (
        0.5 * swap_halves(head_rows).astype(jnp.float32) * swap_halves(rel_rows).astype(jnp.float32)
    ).astype(jnp.bfloat16)
    positive = jnp.sum(query.astype(jnp.float32) * tail_rows.astype(jnp.float32), axis=1)

    own_negs = jnp.take(entity_table, negative_ids, axis=0)
    gathered = lax.all_gather(own_negs, "narrow", axis=0, tiled=True)
    group_neg = gathered.shape[0]
    scores = jnp.einsum("tc,kc->tk", query, gathered, preferred_element_type=jnp.float32)
    loss = jax.nn.softplus(-positive) + jnp.sum(jax.nn.softplus(scores), axis=1) / group_neg
    neg_weights = (jax.nn.sigmoid(scores) / group_neg).astype(jnp.bfloat16)
    pos_weight = -jax.nn.sigmoid(-positive)
    query_grad = pos_weight[:, None] * tail_rows.astype(jnp.float32) + jnp.dot(
        neg_weights, gathered, preferred_element_type=jnp.float32
    )
    tail_grad = pos_weight[:, None] * query.astype(jnp.float32)
    head_grad = 0.5 * swap_halves(query_grad) * rel_rows.astype(jnp.float32)
    rel_part = 0.5 * swap_halves(query_grad) * head_rows.astype(jnp.float32)

    group_query = lax.all_gather(query, "narrow", axis=0, tiled=True)

    send_rel = jnp.einsum(
        "sj,jc->sc",
        rel_place.astype(jnp.bfloat16),
        rel_part.astype(jnp.bfloat16),
        preferred_element_type=jnp.float32,
    ).astype(jnp.bfloat16)
    back_rel = lax.all_to_all(
        send_rel.reshape(device_count, rel_capacity, row_width), AXES, split_axis=0, concat_axis=0, tiled=True
    ).reshape(-1, row_width)
    rel_onehot = (
        rel_ids_in[:, None] == jnp.arange(rel_per_group, dtype=jnp.int32)[None, :]
    ).astype(jnp.bfloat16)
    own_rel_grad = jnp.einsum(
        "sr,sc->rc", rel_onehot, back_rel, preferred_element_type=jnp.float32
    ).astype(jnp.bfloat16)

    ent_grads = jnp.stack([head_grad, tail_grad], axis=1).reshape(2 * triples, row_width)
    send_ent = jnp.einsum(
        "sj,jc->sc", ent_place_bf, ent_grads.astype(jnp.bfloat16), preferred_element_type=jnp.float32
    ).astype(jnp.bfloat16)
    own_rel_grad, send_ent, group_query = lax.optimization_barrier((own_rel_grad, send_ent, group_query))
    relation_grad = lax.all_gather(own_rel_grad, AXES, axis=0, tiled=True)
    back_ent = lax.all_to_all(
        send_ent.reshape(device_count, capacity, row_width), AXES, split_axis=0, concat_axis=0, tiled=True
    ).reshape(-1, row_width)

    own_scores = jnp.einsum("tc,kc->tk", group_query, own_negs, preferred_element_type=jnp.float32)
    own_weights = (jax.nn.sigmoid(own_scores) / group_neg).astype(jnp.bfloat16)
    neg_grad = jnp.einsum("tk,tc->kc", own_weights, group_query, preferred_element_type=jnp.float32)

    entity_iota = jnp.arange(entity_rows, dtype=jnp.int32)[None, :]
    asked_onehot = (asked_ids[:, None] == entity_iota).astype(jnp.bfloat16)
    neg_onehot = (negative_ids[:, None] == entity_iota).astype(jnp.bfloat16)
    entity_grad = jnp.einsum(
        "se,sc->ec", asked_onehot, back_ent, preferred_element_type=jnp.float32
    ) + jnp.einsum(
        "se,sc->ec", neg_onehot, neg_grad.astype(jnp.bfloat16), preferred_element_type=jnp.float32
    )
    return (entity_grad.astype(jnp.bfloat16), relation_grad, loss)


def solution(mesh):
    return jax.shard_map(
        body,
        mesh=mesh,
        in_specs=(
            P(AXES, None),
            P(),
            P(AXES),
            P(AXES, None),
            P(AXES, None),
            P(AXES),
        ),
        out_specs=(P(AXES, None), P(), P(AXES)),
        check_vma=False,
    )
```

```python
import jax
import jax.numpy as jnp
from jax import lax
from jax.sharding import PartitionSpec as P

AXES = ("wide", "narrow")


def swap_halves(rows):
    half_width = rows.shape[-1] // 2
    return jnp.concatenate([rows[..., half_width:], rows[..., :half_width]], axis=-1)


def slot_ranks(targets, count):
    onehot = (targets[:, None] == jnp.arange(count, dtype=jnp.int32)[None, :]).astype(jnp.int32)
    return jnp.sum((jnp.cumsum(onehot, axis=0) - onehot) * onehot, axis=1)


def body(entity_table, relation_table, triple_rel, triple_owners, triple_local, negative_ids):
    wide_count = lax.axis_size("wide")
    narrow_count = lax.axis_size("narrow")
    device_count = wide_count * narrow_count
    triples = triple_rel.shape[0]
    row_width = entity_table.shape[1]
    entity_rows = entity_table.shape[0]
    capacity = max(2, 4 * triples // device_count)
    rel_capacity = max(1, 2 * triples // device_count)
    rel_per_group = relation_table.shape[0] // device_count
    assert rel_per_group <= 256

    owners = triple_owners.reshape(-1)
    local_rows = triple_local.reshape(-1)
    ent_pos = owners * capacity + slot_ranks(owners, device_count)
    rel_group = triple_rel // rel_per_group
    rel_pos = rel_group * rel_capacity + slot_ranks(rel_group, device_count)
    rel_local = triple_rel - rel_group * rel_per_group

    ent_place = jnp.arange(device_count * capacity, dtype=jnp.int32)[:, None] == ent_pos[None, :]
    rel_place = jnp.arange(device_count * rel_capacity, dtype=jnp.int32)[:, None] == rel_pos[None, :]
    send_ent_ids = jnp.sum(jnp.where(ent_place, local_rows[None, :], 0), axis=1)
    recv_ids = lax.all_to_all(
        send_ent_ids.reshape(device_count, capacity), AXES, split_axis=0, concat_axis=0, tiled=True
    )
    asked_ids = recv_ids.reshape(-1)

    entity_iota = jnp.arange(entity_rows, dtype=jnp.int32)[None, :]
    asked_onehot = (asked_ids[:, None] == entity_iota).astype(jnp.bfloat16)
    served = jnp.einsum(
        "se,ec->sc", asked_onehot, entity_table, preferred_element_type=jnp.float32
    ).astype(jnp.bfloat16)
    served = served.reshape(device_count, capacity, row_width)
    got_rows = lax.all_to_all(served, AXES, split_axis=0, concat_axis=0, tiled=True)
    got_rows = got_rows.reshape(device_count * capacity, row_width)
    ent_place_bf = ent_place.astype(jnp.bfloat16)
    fetched = jnp.einsum(
        "sj,sc->jc", ent_place_bf, got_rows, preferred_element_type=jnp.float32
    ).astype(jnp.bfloat16)
    fetched = fetched.reshape(triples, 2, row_width)
    head_rows = fetched[:, 0]
    tail_rows = fetched[:, 1]
    rel_rows = jnp.take(relation_table, triple_rel, axis=0)
    query = (
        0.5 * swap_halves(head_rows).astype(jnp.float32) * swap_halves(rel_rows).astype(jnp.float32)
    ).astype(jnp.bfloat16)
    positive = jnp.sum(query.astype(jnp.float32) * tail_rows.astype(jnp.float32), axis=1)

    own_negs = jnp.take(entity_table, negative_ids, axis=0)
    gathered = lax.all_gather(own_negs, "narrow", axis=0, tiled=True)
    group_neg = gathered.shape[0]
    scores = jnp.einsum("tc,kc->tk", query, gathered, preferred_element_type=jnp.float32)
    loss = jax.nn.softplus(-positive) + jnp.sum(jax.nn.softplus(scores), axis=1) / group_neg
    neg_weights = (jax.nn.sigmoid(scores) / group_neg).astype(jnp.bfloat16)
    pos_weight = -jax.nn.sigmoid(-positive)
    query_grad = pos_weight[:, None] * tail_rows.astype(jnp.float32) + jnp.dot(
        neg_weights, gathered, preferred_element_type=jnp.float32
    )
    tail_grad = pos_weight[:, None] * query.astype(jnp.float32)
    head_grad = 0.5 * swap_halves(query_grad) * rel_rows.astype(jnp.float32)
    rel_part = 0.5 * swap_halves(query_grad) * head_rows.astype(jnp.float32)

    group_query = lax.all_gather(query, "narrow", axis=0, tiled=True)

    send_rel = jnp.einsum(
        "sj,jc->sc",
        rel_place.astype(jnp.bfloat16),
        rel_part.astype(jnp.bfloat16),
        preferred_element_type=jnp.float32,
    ).astype(jnp.bfloat16)
    send_rel_ids = jnp.sum(jnp.where(rel_place, rel_local[None, :], 0), axis=1)
    id_row = jnp.zeros((device_count, 1, row_width), jnp.bfloat16)
    id_row = id_row.at[:, 0, :rel_capacity].set(
        send_rel_ids.reshape(device_count, rel_capacity).astype(jnp.bfloat16)
    )
    send_rel = jnp.concatenate([send_rel.reshape(device_count, rel_capacity, row_width), id_row], axis=1)
    back_rel = lax.all_to_all(send_rel, AXES, split_axis=0, concat_axis=0, tiled=True)
    rel_ids_in = back_rel[:, rel_capacity, :rel_capacity].astype(jnp.int32).reshape(-1)
    back_rel = back_rel[:, :rel_capacity].reshape(-1, row_width)
    rel_onehot = (
        rel_ids_in[:, None] == jnp.arange(rel_per_group, dtype=jnp.int32)[None, :]
    ).astype(jnp.bfloat16)
    own_rel_grad = jnp.einsum(
        "sr,sc->rc", rel_onehot, back_rel, preferred_element_type=jnp.float32
    ).astype(jnp.bfloat16)

    ent_grads = jnp.stack([head_grad, tail_grad], axis=1).reshape(2 * triples, row_width)
    send_ent = jnp.einsum(
        "sj,jc->sc", ent_place_bf, ent_grads.astype(jnp.bfloat16), preferred_element_type=jnp.float32
    ).astype(jnp.bfloat16)
    own_rel_grad, send_ent, group_query = lax.optimization_barrier((own_rel_grad, send_ent, group_query))
    relation_grad = lax.all_gather(own_rel_grad, AXES, axis=0, tiled=True)
    back_ent = lax.all_to_all(
        send_ent.reshape(device_count, capacity, row_width), AXES, split_axis=0, concat_axis=0, tiled=True
    ).reshape(-1, row_width)

    own_scores = jnp.einsum("tc,kc->tk", group_query, own_negs, preferred_element_type=jnp.float32)
    own_weights = (jax.nn.sigmoid(own_scores) / group_neg).astype(jnp.bfloat16)
    neg_grad = jnp.einsum("tk,tc->kc", own_weights, group_query, preferred_element_type=jnp.float32)

    neg_onehot = (negative_ids[:, None] == entity_iota).astype(jnp.bfloat16)
    entity_grad = jnp.einsum(
        "se,sc->ec", asked_onehot, back_ent, preferred_element_type=jnp.float32
    ) + jnp.einsum(
        "se,sc->ec", neg_onehot, neg_grad.astype(jnp.bfloat16), preferred_element_type=jnp.float32
    )
    return (entity_grad.astype(jnp.bfloat16), relation_grad, loss)


def solution(mesh):
    return jax.shard_map(
        body,
        mesh=mesh,
        in_specs=(
            P(AXES, None),
            P(),
            P(AXES),
            P(AXES, None),
            P(AXES, None),
            P(AXES),
        ),
        out_specs=(P(AXES, None), P(), P(AXES)),
        check_vma=False,
    )
```

```python
import jax
import jax.numpy as jnp
from jax import lax
from jax.sharding import PartitionSpec as P

AXES = ("wide", "narrow")


def swap_halves(rows):
    half_width = rows.shape[-1] // 2
    return jnp.concatenate([rows[..., half_width:], rows[..., :half_width]], axis=-1)


def slot_ranks(targets, count):
    onehot = (targets[:, None] == jnp.arange(count, dtype=jnp.int32)[None, :]).astype(jnp.int32)
    return jnp.sum((jnp.cumsum(onehot, axis=0) - onehot) * onehot, axis=1)


def body(entity_table, relation_table, triple_rel, triple_owners, triple_local, negative_ids):
    wide_count = lax.axis_size("wide")
    narrow_count = lax.axis_size("narrow")
    device_count = wide_count * narrow_count
    triples = triple_rel.shape[0]
    row_width = entity_table.shape[1]
    entity_rows = entity_table.shape[0]
    capacity = max(2, 4 * triples // device_count)
    rel_capacity = max(1, 2 * triples // device_count)
    rel_per_group = relation_table.shape[0] // device_count

    owners = triple_owners.reshape(-1)
    local_rows = triple_local.reshape(-1)
    ent_pos = owners * capacity + slot_ranks(owners, device_count)
    rel_group = triple_rel // rel_per_group
    rel_pos = rel_group * rel_capacity + slot_ranks(rel_group, device_count)
    rel_local = triple_rel - rel_group * rel_per_group

    ent_place = jnp.arange(device_count * capacity, dtype=jnp.int32)[:, None] == ent_pos[None, :]
    rel_place = jnp.arange(device_count * rel_capacity, dtype=jnp.int32)[:, None] == rel_pos[None, :]
    send_ent_ids = jnp.sum(jnp.where(ent_place, local_rows[None, :], 0), axis=1)
    send_rel_ids = jnp.sum(jnp.where(rel_place, rel_local[None, :], 0), axis=1)
    send_ids = jnp.stack(
        [
            send_ent_ids.reshape(device_count, capacity),
            jnp.pad(
                send_rel_ids.reshape(device_count, rel_capacity), ((0, 0), (0, capacity - rel_capacity))
            ),
        ],
        axis=1,
    )
    recv_ids = lax.all_to_all(send_ids, AXES, split_axis=0, concat_axis=0, tiled=True)
    asked_ids = recv_ids[:, 0].reshape(-1)
    rel_ids_in = recv_ids[:, 1, :rel_capacity].reshape(-1)

    entity_iota = jnp.arange(entity_rows, dtype=jnp.int32)[None, :]
    asked_onehot = (asked_ids[:, None] == entity_iota).astype(jnp.bfloat16)
    served = jnp.einsum(
        "se,ec->sc", asked_onehot, entity_table, preferred_element_type=jnp.float32
    ).astype(jnp.bfloat16)
    served = served.reshape(device_count, capacity, row_width)
    got_rows = lax.all_to_all(served, AXES, split_axis=0, concat_axis=0, tiled=True)
    got_rows = got_rows.reshape(device_count * capacity, row_width)
    ent_place_bf = ent_place.astype(jnp.bfloat16)
    fetched = jnp.einsum(
        "sj,sc->jc", ent_place_bf, got_rows, preferred_element_type=jnp.float32
    ).astype(jnp.bfloat16)
    fetched = fetched.reshape(triples, 2, row_width)
    head_rows = fetched[:, 0]
    tail_rows = fetched[:, 1]
    rel_rows = jnp.take(relation_table, triple_rel, axis=0)
    query = (
        0.5 * swap_halves(head_rows).astype(jnp.float32) * swap_halves(rel_rows).astype(jnp.float32)
    ).astype(jnp.bfloat16)
    positive = jnp.sum(query.astype(jnp.float32) * tail_rows.astype(jnp.float32), axis=1)

    own_negs = jnp.take(entity_table, negative_ids, axis=0)
    gathered = lax.all_gather(own_negs, "narrow", axis=0, tiled=True)
    group_neg = gathered.shape[0]
    scores = jnp.einsum("tc,kc->tk", query, gathered, preferred_element_type=jnp.float32)
    loss = jax.nn.softplus(-positive) + jnp.sum(jax.nn.softplus(scores), axis=1) / group_neg
    neg_weights = (jax.nn.sigmoid(scores) / group_neg).astype(jnp.bfloat16)
    pos_weight = -jax.nn.sigmoid(-positive)
    query_grad = pos_weight[:, None] * tail_rows.astype(jnp.float32) + jnp.dot(
        neg_weights, gathered, preferred_element_type=jnp.float32
    )
    tail_grad = pos_weight[:, None] * query.astype(jnp.float32)
    head_grad = 0.5 * swap_halves(query_grad) * rel_rows.astype(jnp.float32)
    rel_part = 0.5 * swap_halves(query_grad) * head_rows.astype(jnp.float32)

    group_query = lax.all_gather(query, "narrow", axis=0, tiled=True)

    send_rel = jnp.einsum(
        "sj,jc->sc",
        rel_place.astype(jnp.bfloat16),
        rel_part.astype(jnp.bfloat16),
        preferred_element_type=jnp.float32,
    ).astype(jnp.bfloat16)
    back_rel = lax.all_to_all(
        send_rel.reshape(device_count, rel_capacity, row_width), AXES, split_axis=0, concat_axis=0, tiled=True
    ).reshape(-1, row_width)
    rel_onehot = (
        rel_ids_in[:, None] == jnp.arange(rel_per_group, dtype=jnp.int32)[None, :]
    ).astype(jnp.bfloat16)
    own_rel_grad = jnp.einsum(
        "sr,sc->rc", rel_onehot, back_rel, preferred_element_type=jnp.float32
    ).astype(jnp.bfloat16)

    ent_grads = jnp.stack([head_grad, tail_grad], axis=1).reshape(2 * triples, row_width)
    send_ent = jnp.einsum(
        "sj,jc->sc", ent_place_bf, ent_grads.astype(jnp.bfloat16), preferred_element_type=jnp.float32
    ).astype(jnp.bfloat16)
    own_rel_grad, send_ent, group_query = lax.optimization_barrier((own_rel_grad, send_ent, group_query))
    relation_grad = lax.all_gather(own_rel_grad, AXES, axis=0, tiled=True)
    back_ent = lax.all_to_all(
        send_ent.reshape(device_count, capacity, row_width), AXES, split_axis=0, concat_axis=0, tiled=True
    ).reshape(-1, row_width)

    own_scores = jnp.einsum("tc,kc->tk", group_query, own_negs, preferred_element_type=jnp.float32)
    own_weights = (jax.nn.sigmoid(own_scores) / group_neg).astype(jnp.bfloat16)
    neg_grad = jnp.einsum("tk,tc->kc", own_weights, group_query, preferred_element_type=jnp.float32)

    neg_onehot = (negative_ids[:, None] == entity_iota).astype(jnp.bfloat16)
    entity_grad = jnp.einsum(
        "se,sc->ec", asked_onehot, back_ent, preferred_element_type=jnp.float32
    ) + jnp.einsum(
        "se,sc->ec", neg_onehot, neg_grad.astype(jnp.bfloat16), preferred_element_type=jnp.float32
    )
    return (entity_grad.astype(jnp.bfloat16), relation_grad, loss)


def solution(mesh):
    return jax.shard_map(
        body,
        mesh=mesh,
        in_specs=(
            P(AXES, None),
            P(),
            P(AXES),
            P(AXES, None),
            P(AXES, None),
            P(AXES),
        ),
        out_specs=(P(AXES, None), P(), P(AXES)),
        check_vma=False,
    )
```

```python
import jax
import jax.numpy as jnp
from jax import lax
from jax.sharding import PartitionSpec as P

AXES = ("wide", "narrow")


def swap_halves(rows):
    half_width = rows.shape[-1] // 2
    return jnp.concatenate([rows[..., half_width:], rows[..., :half_width]], axis=-1)


def slot_ranks(targets, count):
    onehot = (targets[:, None] == jnp.arange(count, dtype=jnp.int32)[None, :]).astype(jnp.int32)
    return jnp.sum((jnp.cumsum(onehot, axis=0) - onehot) * onehot, axis=1)


def body(entity_table, relation_table, triple_rel, triple_owners, triple_local, negative_ids):
    wide_count = lax.axis_size("wide")
    narrow_count = lax.axis_size("narrow")
    device_count = wide_count * narrow_count
    triples = triple_rel.shape[0]
    row_width = entity_table.shape[1]
    entity_rows = entity_table.shape[0]
    capacity = max(2, 4 * triples // device_count)
    rel_capacity = max(1, 2 * triples // device_count)
    rel_per_group = relation_table.shape[0] // device_count

    owners = triple_owners.reshape(-1)
    local_rows = triple_local.reshape(-1)
    ent_pos = owners * capacity + slot_ranks(owners, device_count)
    rel_group = triple_rel // rel_per_group
    rel_pos = rel_group * rel_capacity + slot_ranks(rel_group, device_count)
    rel_local = triple_rel - rel_group * rel_per_group

    ent_place = jnp.arange(device_count * capacity, dtype=jnp.int32)[:, None] == ent_pos[None, :]
    rel_place = jnp.arange(device_count * rel_capacity, dtype=jnp.int32)[:, None] == rel_pos[None, :]
    send_ent_ids = jnp.sum(jnp.where(ent_place, local_rows[None, :], 0), axis=1)
    send_rel_ids = jnp.sum(jnp.where(rel_place, rel_local[None, :], 0), axis=1)
    send_ids = jnp.stack(
        [
            send_ent_ids.reshape(device_count, capacity),
            jnp.pad(
                send_rel_ids.reshape(device_count, rel_capacity), ((0, 0), (0, capacity - rel_capacity))
            ),
        ],
        axis=1,
    )
    recv_ids = lax.all_to_all(send_ids, AXES, split_axis=0, concat_axis=0, tiled=True)
    asked_ids = recv_ids[:, 0].reshape(-1)
    rel_ids_in = recv_ids[:, 1, :rel_capacity].reshape(-1)

    entity_iota = jnp.arange(entity_rows, dtype=jnp.int32)[None, :]
    asked_onehot = (asked_ids[:, None] == entity_iota).astype(jnp.bfloat16)
    served = jnp.einsum(
        "se,ec->sc", asked_onehot, entity_table, preferred_element_type=jnp.float32
    ).astype(jnp.bfloat16)
    served = served.reshape(device_count, capacity, row_width)
    got_rows = lax.all_to_all(served, AXES, split_axis=0, concat_axis=0, tiled=True)
    got_rows = got_rows.reshape(device_count * capacity, row_width)
    ent_place_bf = ent_place.astype(jnp.bfloat16)
    fetched = jnp.einsum(
        "sj,sc->jc", ent_place_bf, got_rows, preferred_element_type=jnp.float32
    ).astype(jnp.bfloat16)
    fetched = fetched.reshape(triples, 2, row_width)
    head_rows = fetched[:, 0]
    tail_rows = fetched[:, 1]
    rel_rows = jnp.take(relation_table, triple_rel, axis=0)
    query = (
        0.5 * swap_halves(head_rows).astype(jnp.float32) * swap_halves(rel_rows).astype(jnp.float32)
    ).astype(jnp.bfloat16)
    positive = jnp.sum(query.astype(jnp.float32) * tail_rows.astype(jnp.float32), axis=1)

    own_negs = jnp.take(entity_table, negative_ids, axis=0)
    gathered = lax.all_gather(own_negs, "narrow", axis=0, tiled=True)
    group_neg = gathered.shape[0]
    scores = jnp.einsum("tc,kc->tk", query, gathered, preferred_element_type=jnp.float32)
    loss = jax.nn.softplus(-positive) + jnp.sum(jax.nn.softplus(scores), axis=1) / group_neg
    neg_weights = (jax.nn.sigmoid(scores) / group_neg).astype(jnp.bfloat16)
    pos_weight = -jax.nn.sigmoid(-positive)
    query_grad = pos_weight[:, None] * tail_rows.astype(jnp.float32) + jnp.dot(
        neg_weights, gathered, preferred_element_type=jnp.float32
    )
    tail_grad = pos_weight[:, None] * query.astype(jnp.float32)
    head_grad = 0.5 * swap_halves(query_grad) * rel_rows.astype(jnp.float32)
    rel_part = 0.5 * swap_halves(query_grad) * head_rows.astype(jnp.float32)

    group_query = lax.all_gather(query, "narrow", axis=0, tiled=True)

    send_rel = jnp.einsum(
        "sj,jc->sc",
        rel_place.astype(jnp.bfloat16),
        rel_part.astype(jnp.bfloat16),
        preferred_element_type=jnp.float32,
    ).astype(jnp.bfloat16)
    back_rel = lax.all_to_all(
        send_rel.reshape(device_count, rel_capacity, row_width), AXES, split_axis=0, concat_axis=0, tiled=True
    ).reshape(-1, row_width)
    rel_onehot = (
        rel_ids_in[:, None] == jnp.arange(rel_per_group, dtype=jnp.int32)[None, :]
    ).astype(jnp.bfloat16)
    own_rel_grad = jnp.einsum(
        "sr,sc->rc", rel_onehot, back_rel, preferred_element_type=jnp.float32
    ).astype(jnp.bfloat16)

    ent_grads = jnp.stack([head_grad, tail_grad], axis=1).reshape(2 * triples, row_width)
    send_ent = jnp.einsum(
        "sj,jc->sc", ent_place_bf, ent_grads.astype(jnp.bfloat16), preferred_element_type=jnp.float32
    ).astype(jnp.bfloat16)
    own_rel_grad, send_ent, group_query = lax.optimization_barrier((own_rel_grad, send_ent, group_query))
    core = lax.axis_index("narrow") % 2
    pair_perm = [(i, i ^ 1) for i in range(narrow_count)]
    core_groups = [[d for d in range(device_count) if d % 2 == k] for k in range(2)]
    mine = lax.all_gather(own_rel_grad, AXES, axis=0, tiled=False, axis_index_groups=core_groups)
    other = lax.ppermute(mine, "narrow", pair_perm)
    parity = jnp.arange(2, dtype=jnp.int32)[None, :, None, None]
    relation_grad = jnp.where(parity == core, mine[:, None], other[:, None]).reshape(-1, row_width)
    back_ent = lax.all_to_all(
        send_ent.reshape(device_count, capacity, row_width), AXES, split_axis=0, concat_axis=0, tiled=True
    ).reshape(-1, row_width)

    own_scores = jnp.einsum("tc,kc->tk", group_query, own_negs, preferred_element_type=jnp.float32)
    own_weights = (jax.nn.sigmoid(own_scores) / group_neg).astype(jnp.bfloat16)
    neg_grad = jnp.einsum("tk,tc->kc", own_weights, group_query, preferred_element_type=jnp.float32)

    neg_onehot = (negative_ids[:, None] == entity_iota).astype(jnp.bfloat16)
    entity_grad = jnp.einsum(
        "se,sc->ec", asked_onehot, back_ent, preferred_element_type=jnp.float32
    ) + jnp.einsum(
        "se,sc->ec", neg_onehot, neg_grad.astype(jnp.bfloat16), preferred_element_type=jnp.float32
    )
    return (entity_grad.astype(jnp.bfloat16), relation_grad, loss)


def solution(mesh):
    return jax.shard_map(
        body,
        mesh=mesh,
        in_specs=(
            P(AXES, None),
            P(),
            P(AXES),
            P(AXES, None),
            P(AXES, None),
            P(AXES),
        ),
        out_specs=(P(AXES, None), P(), P(AXES)),
        check_vma=False,
    )
```

```python
import jax
import jax.numpy as jnp
from jax import lax
from jax.sharding import PartitionSpec as P

AXES = ("wide", "narrow")


def swap_halves(rows):
    half_width = rows.shape[-1] // 2
    return jnp.concatenate([rows[..., half_width:], rows[..., :half_width]], axis=-1)


def slot_ranks(targets):
    index = jnp.arange(targets.shape[0], dtype=jnp.int32)
    earlier_same = (targets[:, None] == targets[None, :]) & (index[:, None] < index[None, :])
    return jnp.sum(earlier_same.astype(jnp.int32), axis=0)


def body(entity_table, relation_table, triple_rel, triple_owners, triple_local, negative_ids):
    wide_count = lax.axis_size("wide")
    narrow_count = lax.axis_size("narrow")
    device_count = wide_count * narrow_count
    triples = triple_rel.shape[0]
    row_width = entity_table.shape[1]
    entity_rows = entity_table.shape[0]
    capacity = max(2, 4 * triples // device_count)
    rel_capacity = max(1, 2 * triples // device_count)
    rel_per_group = relation_table.shape[0] // device_count

    owners = jnp.concatenate([triple_owners[:, 0], triple_owners[:, 1]])
    local_rows = jnp.concatenate([triple_local[:, 0], triple_local[:, 1]])
    ent_pos = owners * capacity + slot_ranks(owners)
    rel_group = triple_rel // rel_per_group
    rel_pos = rel_group * rel_capacity + slot_ranks(rel_group)
    rel_local = triple_rel - rel_group * rel_per_group

    ent_place = jnp.arange(device_count * capacity, dtype=jnp.int32)[:, None] == ent_pos[None, :]
    rel_place = jnp.arange(device_count * rel_capacity, dtype=jnp.int32)[:, None] == rel_pos[None, :]
    send_ent_ids = jnp.sum(jnp.where(ent_place, local_rows[None, :], 0), axis=1)
    send_rel_ids = jnp.sum(jnp.where(rel_place, rel_local[None, :], 0), axis=1)
    send_ids = jnp.stack(
        [
            send_ent_ids.reshape(device_count, capacity),
            jnp.pad(
                send_rel_ids.reshape(device_count, rel_capacity), ((0, 0), (0, capacity - rel_capacity))
            ),
        ],
        axis=1,
    )
    recv_ids = lax.all_to_all(send_ids, AXES, split_axis=0, concat_axis=0, tiled=True)
    asked_ids = recv_ids[:, 0].reshape(-1)
    rel_ids_in = recv_ids[:, 1, :rel_capacity].reshape(-1)

    entity_iota = jnp.arange(entity_rows, dtype=jnp.int32)[None, :]
    asked_onehot = (asked_ids[:, None] == entity_iota).astype(jnp.bfloat16)
    served = jnp.einsum(
        "se,ec->sc", asked_onehot, entity_table, preferred_element_type=jnp.float32
    ).astype(jnp.bfloat16)
    served = served.reshape(device_count, capacity, row_width)
    got_rows = lax.all_to_all(served, AXES, split_axis=0, concat_axis=0, tiled=True)
    got_rows = got_rows.reshape(device_count * capacity, row_width)
    ent_place_bf = ent_place.astype(jnp.bfloat16)
    fetched = jnp.einsum(
        "sj,sc->jc", ent_place_bf, got_rows, preferred_element_type=jnp.float32
    ).astype(jnp.bfloat16)
    head_rows = fetched[:triples]
    tail_rows = fetched[triples:]
    rel_rows = jnp.take(relation_table, triple_rel, axis=0)
    query = (
        0.5 * swap_halves(head_rows).astype(jnp.float32) * swap_halves(rel_rows).astype(jnp.float32)
    ).astype(jnp.bfloat16)
    positive = jnp.sum(query.astype(jnp.float32) * tail_rows.astype(jnp.float32), axis=1)

    own_negs = jnp.take(entity_table, negative_ids, axis=0)
    gathered = lax.all_gather(own_negs, "narrow", axis=0, tiled=True)
    group_neg = gathered.shape[0]
    scores = jnp.einsum("tc,kc->tk", query, gathered, preferred_element_type=jnp.float32)
    loss = jax.nn.softplus(-positive) + jnp.sum(jax.nn.softplus(scores), axis=1) / group_neg
    neg_weights = (jax.nn.sigmoid(scores) / group_neg).astype(jnp.bfloat16)
    pos_weight = -jax.nn.sigmoid(-positive)
    query_grad = pos_weight[:, None] * tail_rows.astype(jnp.float32) + jnp.dot(
        neg_weights, gathered, preferred_element_type=jnp.float32
    )
    tail_grad = pos_weight[:, None] * query.astype(jnp.float32)
    head_grad = 0.5 * swap_halves(query_grad) * rel_rows.astype(jnp.float32)
    rel_part = 0.5 * swap_halves(query_grad) * head_rows.astype(jnp.float32)

    group_query = lax.all_gather(query, "narrow", axis=0, tiled=True)

    send_rel = jnp.einsum(
        "sj,jc->sc",
        rel_place.astype(jnp.bfloat16),
        rel_part.astype(jnp.bfloat16),
        preferred_element_type=jnp.float32,
    ).astype(jnp.bfloat16)
    back_rel = lax.all_to_all(
        send_rel.reshape(device_count, rel_capacity, row_width), AXES, split_axis=0, concat_axis=0, tiled=True
    ).reshape(-1, row_width)
    rel_onehot = (
        rel_ids_in[:, None] == jnp.arange(rel_per_group, dtype=jnp.int32)[None, :]
    ).astype(jnp.bfloat16)
    own_rel_grad = jnp.einsum(
        "sr,sc->rc", rel_onehot, back_rel, preferred_element_type=jnp.float32
    ).astype(jnp.bfloat16)

    ent_grads = jnp.concatenate([head_grad, tail_grad], axis=0)
    send_ent = jnp.einsum(
        "sj,jc->sc", ent_place_bf, ent_grads.astype(jnp.bfloat16), preferred_element_type=jnp.float32
    ).astype(jnp.bfloat16)
    own_rel_grad, send_ent, group_query = lax.optimization_barrier((own_rel_grad, send_ent, group_query))
    relation_grad = lax.all_gather(own_rel_grad, AXES, axis=0, tiled=True)
    back_ent = lax.all_to_all(
        send_ent.reshape(device_count, capacity, row_width), AXES, split_axis=0, concat_axis=0, tiled=True
    ).reshape(-1, row_width)

    own_scores = jnp.einsum("tc,kc->tk", group_query, own_negs, preferred_element_type=jnp.float32)
    own_weights = (jax.nn.sigmoid(own_scores) / group_neg).astype(jnp.bfloat16)
    neg_grad = jnp.einsum("tk,tc->kc", own_weights, group_query, preferred_element_type=jnp.float32)

    neg_onehot = (negative_ids[:, None] == entity_iota).astype(jnp.bfloat16)
    entity_grad = jnp.einsum(
        "se,sc->ec", asked_onehot, back_ent, preferred_element_type=jnp.float32
    ) + jnp.einsum(
        "se,sc->ec", neg_onehot, neg_grad.astype(jnp.bfloat16), preferred_element_type=jnp.float32
    )
    return (entity_grad.astype(jnp.bfloat16), relation_grad, loss)


def solution(mesh):
    return jax.shard_map(
        body,
        mesh=mesh,
        in_specs=(
            P(AXES, None),
            P(),
            P(AXES),
            P(AXES, None),
            P(AXES, None),
            P(AXES),
        ),
        out_specs=(P(AXES, None), P(), P(AXES)),
        check_vma=False,
    )
```

```python
import jax
import jax.numpy as jnp
from jax import lax
from jax.sharding import PartitionSpec as P

AXES = ("wide", "narrow")


def swap_halves(rows):
    half_width = rows.shape[-1] // 2
    return jnp.concatenate([rows[..., half_width:], rows[..., :half_width]], axis=-1)


def slot_ranks(targets):
    index = jnp.arange(targets.shape[0], dtype=jnp.int32)
    earlier_same = (targets[:, None] == targets[None, :]) & (index[:, None] < index[None, :])
    return jnp.sum(earlier_same.astype(jnp.int32), axis=0)


def body(entity_table, relation_table, triple_rel, triple_owners, triple_local, negative_ids):
    wide_count = lax.axis_size("wide")
    narrow_count = lax.axis_size("narrow")
    device_count = wide_count * narrow_count
    triples = triple_rel.shape[0]
    row_width = entity_table.shape[1]
    entity_rows = entity_table.shape[0]
    capacity = max(2, 4 * triples // device_count)
    rel_capacity = max(1, 2 * triples // device_count)
    rel_per_group = relation_table.shape[0] // device_count

    owners = jnp.concatenate([triple_owners[:, 0], triple_owners[:, 1]])
    local_rows = jnp.concatenate([triple_local[:, 0], triple_local[:, 1]])
    ent_pos = owners * capacity + slot_ranks(owners)
    rel_group = triple_rel // rel_per_group
    rel_pos = rel_group * rel_capacity + slot_ranks(rel_group)
    rel_local = triple_rel - rel_group * rel_per_group

    ent_place = jnp.arange(device_count * capacity, dtype=jnp.int32)[:, None] == ent_pos[None, :]
    rel_place = jnp.arange(device_count * rel_capacity, dtype=jnp.int32)[:, None] == rel_pos[None, :]
    send_ent_ids = jnp.sum(jnp.where(ent_place, local_rows[None, :], 0), axis=1)
    send_rel_ids = jnp.sum(jnp.where(rel_place, rel_local[None, :], 0), axis=1)
    send_ids = jnp.stack(
        [
            send_ent_ids.reshape(device_count, capacity),
            jnp.pad(
                send_rel_ids.reshape(device_count, rel_capacity), ((0, 0), (0, capacity - rel_capacity))
            ),
        ],
        axis=1,
    )
    recv_ids = lax.all_to_all(send_ids, AXES, split_axis=0, concat_axis=0, tiled=True)
    asked_ids = recv_ids[:, 0].reshape(-1)
    rel_ids_in = recv_ids[:, 1, :rel_capacity].reshape(-1)

    entity_iota = jnp.arange(entity_rows, dtype=jnp.int32)[None, :]
    asked_onehot = (asked_ids[:, None] == entity_iota).astype(jnp.bfloat16)
    served = jnp.einsum(
        "se,ec->sc", asked_onehot, entity_table, preferred_element_type=jnp.float32
    ).astype(jnp.bfloat16)
    served = served.reshape(device_count, capacity, row_width)
    got_rows = lax.all_to_all(served, AXES, split_axis=0, concat_axis=0, tiled=True)
    got_rows = got_rows.reshape(device_count * capacity, row_width)
    ent_place_bf = ent_place.astype(jnp.bfloat16)
    ent_pick = (ent_pos[:, None] == jnp.arange(device_count * capacity, dtype=jnp.int32)[None, :]).astype(
        jnp.bfloat16
    )
    fetched = jnp.einsum(
        "js,sc->jc", ent_pick, got_rows, preferred_element_type=jnp.float32
    ).astype(jnp.bfloat16)
    head_rows = fetched[:triples]
    tail_rows = fetched[triples:]
    rel_rows = jnp.take(relation_table, triple_rel, axis=0)
    query = (
        0.5 * swap_halves(head_rows).astype(jnp.float32) * swap_halves(rel_rows).astype(jnp.float32)
    ).astype(jnp.bfloat16)
    positive = jnp.sum(query.astype(jnp.float32) * tail_rows.astype(jnp.float32), axis=1)

    own_negs = jnp.take(entity_table, negative_ids, axis=0)
    gathered = lax.all_gather(own_negs, "narrow", axis=0, tiled=True)
    group_neg = gathered.shape[0]
    scores = jnp.einsum("tc,kc->tk", query, gathered, preferred_element_type=jnp.float32)
    loss = jax.nn.softplus(-positive) + jnp.sum(jax.nn.softplus(scores), axis=1) / group_neg
    neg_weights = (jax.nn.sigmoid(scores) / group_neg).astype(jnp.bfloat16)
    pos_weight = -jax.nn.sigmoid(-positive)
    query_grad = pos_weight[:, None] * tail_rows.astype(jnp.float32) + jnp.dot(
        neg_weights, gathered, preferred_element_type=jnp.float32
    )
    tail_grad = pos_weight[:, None] * query.astype(jnp.float32)
    head_grad = 0.5 * swap_halves(query_grad) * rel_rows.astype(jnp.float32)
    rel_part = 0.5 * swap_halves(query_grad) * head_rows.astype(jnp.float32)

    group_query = lax.all_gather(query, "narrow", axis=0, tiled=True)

    send_rel = jnp.einsum(
        "sj,jc->sc",
        rel_place.astype(jnp.bfloat16),
        rel_part.astype(jnp.bfloat16),
        preferred_element_type=jnp.float32,
    ).astype(jnp.bfloat16)
    back_rel = lax.all_to_all(
        send_rel.reshape(device_count, rel_capacity, row_width), AXES, split_axis=0, concat_axis=0, tiled=True
    ).reshape(-1, row_width)
    rel_onehot = (
        jnp.arange(rel_per_group, dtype=jnp.int32)[:, None] == rel_ids_in[None, :]
    ).astype(jnp.bfloat16)
    own_rel_grad = jnp.einsum(
        "rs,sc->rc", rel_onehot, back_rel, preferred_element_type=jnp.float32
    ).astype(jnp.bfloat16)

    ent_grads = jnp.concatenate([head_grad, tail_grad], axis=0)
    send_ent = jnp.einsum(
        "sj,jc->sc", ent_place_bf, ent_grads.astype(jnp.bfloat16), preferred_element_type=jnp.float32
    ).astype(jnp.bfloat16)
    own_rel_grad, send_ent, group_query = lax.optimization_barrier((own_rel_grad, send_ent, group_query))
    relation_grad = lax.all_gather(own_rel_grad, AXES, axis=0, tiled=True)
    back_ent = lax.all_to_all(
        send_ent.reshape(device_count, capacity, row_width), AXES, split_axis=0, concat_axis=0, tiled=True
    ).reshape(-1, row_width)

    own_scores = jnp.einsum("tc,kc->tk", group_query, own_negs, preferred_element_type=jnp.float32)
    own_weights = (jax.nn.sigmoid(own_scores) / group_neg).astype(jnp.bfloat16)
    neg_grad = jnp.einsum("tk,tc->kc", own_weights, group_query, preferred_element_type=jnp.float32)

    neg_onehot = (negative_ids[:, None] == entity_iota).astype(jnp.bfloat16)
    entity_grad = jnp.einsum(
        "se,sc->ec", asked_onehot, back_ent, preferred_element_type=jnp.float32
    ) + jnp.einsum(
        "se,sc->ec", neg_onehot, neg_grad.astype(jnp.bfloat16), preferred_element_type=jnp.float32
    )
    return (entity_grad.astype(jnp.bfloat16), relation_grad, loss)


def solution(mesh):
    return jax.shard_map(
        body,
        mesh=mesh,
        in_specs=(
            P(AXES, None),
            P(),
            P(AXES),
            P(AXES, None),
            P(AXES, None),
            P(AXES),
        ),
        out_specs=(P(AXES, None), P(), P(AXES)),
        check_vma=False,
    )
```

```python
import jax
import jax.numpy as jnp
from jax import lax
from jax.sharding import PartitionSpec as P

AXES = ("wide", "narrow")


def swap_halves(rows):
    half_width = rows.shape[-1] // 2
    return jnp.concatenate([rows[..., half_width:], rows[..., :half_width]], axis=-1)


def slot_ranks(targets):
    index = jnp.arange(targets.shape[0], dtype=jnp.int32)
    earlier_same = (targets[:, None] == targets[None, :]) & (index[:, None] < index[None, :])
    return jnp.sum(earlier_same.astype(jnp.int32), axis=0)


def body(entity_table, relation_table, triple_rel, triple_owners, triple_local, negative_ids):
    wide_count = lax.axis_size("wide")
    narrow_count = lax.axis_size("narrow")
    device_count = wide_count * narrow_count
    triples = triple_rel.shape[0]
    row_width = entity_table.shape[1]
    entity_rows = entity_table.shape[0]
    capacity = max(2, 4 * triples // device_count)
    rel_capacity = max(1, 2 * triples // device_count)
    rel_per_group = relation_table.shape[0] // device_count

    owners = jnp.concatenate([triple_owners[:, 0], triple_owners[:, 1]])
    local_rows = jnp.concatenate([triple_local[:, 0], triple_local[:, 1]])
    ent_pos = owners * capacity + slot_ranks(owners)
    rel_group = triple_rel // rel_per_group
    rel_pos = rel_group * rel_capacity + slot_ranks(rel_group)
    rel_local = triple_rel - rel_group * rel_per_group

    ent_place = jnp.arange(device_count * capacity, dtype=jnp.int32)[:, None] == ent_pos[None, :]
    rel_place = jnp.arange(device_count * rel_capacity, dtype=jnp.int32)[:, None] == rel_pos[None, :]
    send_ent_ids = jnp.sum(jnp.where(ent_place, local_rows[None, :], 0), axis=1)
    send_rel_ids = jnp.sum(jnp.where(rel_place, rel_local[None, :], 0), axis=1)
    send_ids = jnp.stack(
        [
            send_ent_ids.reshape(device_count, capacity),
            jnp.pad(
                send_rel_ids.reshape(device_count, rel_capacity), ((0, 0), (0, capacity - rel_capacity))
            ),
        ],
        axis=1,
    )
    recv_ids = lax.all_to_all(send_ids, AXES, split_axis=0, concat_axis=0, tiled=True)
    asked_ids = recv_ids[:, 0].reshape(-1)
    rel_ids_in = recv_ids[:, 1, :rel_capacity].reshape(-1)

    entity_iota = jnp.arange(entity_rows, dtype=jnp.int32)[None, :]
    asked_onehot = (asked_ids[:, None] == entity_iota).astype(jnp.bfloat16)
    served = jnp.einsum(
        "se,ec->sc", asked_onehot, entity_table, preferred_element_type=jnp.float32
    ).astype(jnp.bfloat16)
    served = served.reshape(device_count, capacity, row_width)
    got_rows = lax.all_to_all(served, AXES, split_axis=0, concat_axis=0, tiled=True)
    got_rows = got_rows.reshape(device_count * capacity, row_width)
    ent_place_bf = ent_place.astype(jnp.bfloat16)
    fetched = jnp.einsum(
        "sj,sc->jc", ent_place_bf, got_rows, preferred_element_type=jnp.float32
    ).astype(jnp.bfloat16)
    head_rows = fetched[:triples]
    tail_rows = fetched[triples:]
    rel_rows = jnp.take(relation_table, triple_rel, axis=0)
    query = (
        0.5 * swap_halves(head_rows).astype(jnp.float32) * swap_halves(rel_rows).astype(jnp.float32)
    ).astype(jnp.bfloat16)
    positive = jnp.sum(query.astype(jnp.float32) * tail_rows.astype(jnp.float32), axis=1)

    own_negs = jnp.take(entity_table, negative_ids, axis=0)
    gathered = lax.all_gather(own_negs, "narrow", axis=0, tiled=True)
    group_neg = gathered.shape[0]
    scores = jnp.einsum("tc,kc->tk", query, gathered, preferred_element_type=jnp.float32)
    loss = jax.nn.softplus(-positive) + jnp.sum(jax.nn.softplus(scores), axis=1) / group_neg
    neg_weights = (jax.nn.sigmoid(scores) / group_neg).astype(jnp.bfloat16)
    pos_weight = -jax.nn.sigmoid(-positive)
    query_grad = pos_weight[:, None] * tail_rows.astype(jnp.float32) + jnp.dot(
        neg_weights, gathered, preferred_element_type=jnp.float32
    )
    tail_grad = pos_weight[:, None] * query.astype(jnp.float32)
    head_grad = 0.5 * swap_halves(query_grad) * rel_rows.astype(jnp.float32)
    rel_part = 0.5 * swap_halves(query_grad) * head_rows.astype(jnp.float32)

    group_query = lax.all_gather(query, "narrow", axis=0, tiled=True)

    send_rel = jnp.einsum(
        "sj,jc->sc",
        rel_place.astype(jnp.bfloat16),
        rel_part.astype(jnp.bfloat16),
        preferred_element_type=jnp.float32,
    ).astype(jnp.bfloat16)
    back_rel = lax.all_to_all(
        send_rel.reshape(device_count, rel_capacity, row_width), AXES, split_axis=0, concat_axis=0, tiled=True
    ).reshape(-1, row_width)
    rel_onehot = (
        rel_ids_in[:, None] == jnp.arange(rel_per_group, dtype=jnp.int32)[None, :]
    ).astype(jnp.bfloat16)
    own_rel_grad = jnp.einsum(
        "sr,sc->rc", rel_onehot, back_rel, preferred_element_type=jnp.float32
    ).astype(jnp.bfloat16)

    ent_grads = jnp.concatenate([head_grad, tail_grad], axis=0)
    send_ent = jnp.einsum(
        "sj,jc->sc", ent_place_bf, ent_grads.astype(jnp.bfloat16), preferred_element_type=jnp.float32
    ).astype(jnp.bfloat16)
    own_rel_grad, send_ent, group_query = lax.optimization_barrier((own_rel_grad, send_ent, group_query))
    relation_grad = lax.all_gather(own_rel_grad, AXES, axis=0, tiled=True)
    own_scores = jnp.einsum("tc,kc->tk", group_query, own_negs, preferred_element_type=jnp.float32)
    own_weights = (jax.nn.sigmoid(own_scores) / group_neg).astype(jnp.bfloat16)
    neg_grad = jnp.einsum("tk,tc->kc", own_weights, group_query, preferred_element_type=jnp.float32)
    neg_onehot = (negative_ids[:, None] == entity_iota).astype(jnp.bfloat16)
    neg_part = jnp.einsum(
        "se,sc->ec", neg_onehot, neg_grad.astype(jnp.bfloat16), preferred_element_type=jnp.float32
    )
    send_ent, neg_part = lax.optimization_barrier((send_ent, neg_part))
    back_ent = lax.all_to_all(
        send_ent.reshape(device_count, capacity, row_width), AXES, split_axis=0, concat_axis=0, tiled=True
    ).reshape(-1, row_width)
    entity_grad = (
        jnp.einsum("se,sc->ec", asked_onehot, back_ent, preferred_element_type=jnp.float32) + neg_part
    )
    return (entity_grad.astype(jnp.bfloat16), relation_grad, loss)


def solution(mesh):
    return jax.shard_map(
        body,
        mesh=mesh,
        in_specs=(
            P(AXES, None),
            P(),
            P(AXES),
            P(AXES, None),
            P(AXES, None),
            P(AXES),
        ),
        out_specs=(P(AXES, None), P(), P(AXES)),
        check_vma=False,
    )
```

```python
import jax
import jax.numpy as jnp
from jax import lax
from jax.sharding import PartitionSpec as P

AXES = ("wide", "narrow")


def swap_halves(rows):
    half_width = rows.shape[-1] // 2
    return jnp.concatenate([rows[..., half_width:], rows[..., :half_width]], axis=-1)


def slot_ranks(targets):
    index = jnp.arange(targets.shape[0], dtype=jnp.int32)
    earlier_same = (targets[:, None] == targets[None, :]) & (index[:, None] < index[None, :])
    return jnp.sum(earlier_same.astype(jnp.int32), axis=0)


def body(entity_table, relation_table, triple_rel, triple_owners, triple_local, negative_ids):
    wide_count = lax.axis_size("wide")
    narrow_count = lax.axis_size("narrow")
    device_count = wide_count * narrow_count
    triples = triple_rel.shape[0]
    row_width = entity_table.shape[1]
    entity_rows = entity_table.shape[0]
    capacity = max(2, 4 * triples // device_count)
    rel_capacity = max(1, 2 * triples // device_count)
    rel_per_group = relation_table.shape[0] // device_count

    owners = jnp.concatenate([triple_owners[:, 0], triple_owners[:, 1]])
    local_rows = jnp.concatenate([triple_local[:, 0], triple_local[:, 1]])
    ent_pos = owners * capacity + slot_ranks(owners)
    rel_group = triple_rel // rel_per_group
    rel_pos = rel_group * rel_capacity + slot_ranks(rel_group)
    rel_local = triple_rel - rel_group * rel_per_group

    ent_place = jnp.arange(device_count * capacity, dtype=jnp.int32)[:, None] == ent_pos[None, :]
    rel_place = jnp.arange(device_count * rel_capacity, dtype=jnp.int32)[:, None] == rel_pos[None, :]
    send_ent_ids = jnp.sum(jnp.where(ent_place, local_rows[None, :], 0), axis=1)
    send_rel_ids = jnp.sum(jnp.where(rel_place, rel_local[None, :], 0), axis=1)
    send_ids = jnp.stack(
        [
            send_ent_ids.reshape(device_count, capacity),
            jnp.pad(
                send_rel_ids.reshape(device_count, rel_capacity), ((0, 0), (0, capacity - rel_capacity))
            ),
        ],
        axis=1,
    )
    recv_ids = lax.all_to_all(send_ids, AXES, split_axis=0, concat_axis=0, tiled=True)
    asked_ids = recv_ids[:, 0].reshape(-1)
    rel_ids_in = recv_ids[:, 1, :rel_capacity].reshape(-1)

    entity_iota = jnp.arange(entity_rows, dtype=jnp.int32)[None, :]
    asked_onehot = (asked_ids[:, None] == entity_iota).astype(jnp.bfloat16)
    served = jnp.einsum(
        "se,ec->sc", asked_onehot, entity_table, preferred_element_type=jnp.float32
    ).astype(jnp.bfloat16)
    served = served.reshape(device_count, capacity, row_width)
    got_rows = lax.all_to_all(served, AXES, split_axis=0, concat_axis=0, tiled=True)
    got_rows = got_rows.reshape(device_count * capacity, row_width)
    ent_place_bf = ent_place.astype(jnp.bfloat16)
    fetched = jnp.einsum(
        "sj,sc->jc", ent_place_bf, got_rows, preferred_element_type=jnp.float32
    ).astype(jnp.bfloat16)
    head_rows = fetched[:triples]
    tail_rows = fetched[triples:]
    rel_rows = jnp.take(relation_table, triple_rel, axis=0)
    query = (
        0.5 * swap_halves(head_rows).astype(jnp.float32) * swap_halves(rel_rows).astype(jnp.float32)
    ).astype(jnp.bfloat16)
    positive = jnp.sum(query.astype(jnp.float32) * tail_rows.astype(jnp.float32), axis=1)

    own_negs = jnp.take(entity_table, negative_ids, axis=0)
    gathered = lax.all_gather(own_negs, "narrow", axis=0, tiled=True)
    group_neg = gathered.shape[0]
    scores = jnp.einsum("tc,kc->tk", query, gathered, preferred_element_type=jnp.float32)
    loss = jax.nn.softplus(-positive) + jnp.sum(jax.nn.softplus(scores), axis=1) / group_neg
    neg_weights = (jax.nn.sigmoid(scores) / group_neg).astype(jnp.bfloat16)
    pos_weight = -jax.nn.sigmoid(-positive)
    query_grad = pos_weight[:, None] * tail_rows.astype(jnp.float32) + jnp.dot(
        neg_weights, gathered, preferred_element_type=jnp.float32
    )
    tail_grad = pos_weight[:, None] * query.astype(jnp.float32)
    head_grad = 0.5 * swap_halves(query_grad) * rel_rows.astype(jnp.float32)
    rel_part = 0.5 * swap_halves(query_grad) * head_rows.astype(jnp.float32)

    group_query = lax.all_gather(query, "narrow", axis=0, tiled=True)

    send_rel = jnp.einsum(
        "sj,jc->sc",
        rel_place.astype(jnp.bfloat16),
        rel_part.astype(jnp.bfloat16),
        preferred_element_type=jnp.float32,
    ).astype(jnp.bfloat16)
    back_rel = lax.all_to_all(
        send_rel.reshape(device_count, rel_capacity, row_width), AXES, split_axis=0, concat_axis=0, tiled=True
    ).reshape(-1, row_width)
    rel_onehot = (
        rel_ids_in[:, None] == jnp.arange(rel_per_group, dtype=jnp.int32)[None, :]
    ).astype(jnp.bfloat16)
    own_rel_grad = jnp.einsum(
        "sr,sc->rc", rel_onehot, back_rel, preferred_element_type=jnp.float32
    ).astype(jnp.bfloat16)

    ent_grads = jnp.concatenate([head_grad, tail_grad], axis=0)
    send_ent = jnp.einsum(
        "sj,jc->sc", ent_place_bf, ent_grads.astype(jnp.bfloat16), preferred_element_type=jnp.float32
    ).astype(jnp.bfloat16)
    own_rel_grad, send_ent, group_query = lax.optimization_barrier((own_rel_grad, send_ent, group_query))
    relation_grad = lax.all_gather(own_rel_grad.reshape(-1), AXES, axis=0, tiled=True).reshape(-1, row_width)
    back_ent = lax.all_to_all(
        send_ent.reshape(device_count, capacity, row_width), AXES, split_axis=0, concat_axis=0, tiled=True
    ).reshape(-1, row_width)

    own_scores = jnp.einsum("tc,kc->tk", group_query, own_negs, preferred_element_type=jnp.float32)
    own_weights = (jax.nn.sigmoid(own_scores) / group_neg).astype(jnp.bfloat16)
    neg_grad = jnp.einsum("tk,tc->kc", own_weights, group_query, preferred_element_type=jnp.float32)

    neg_onehot = (negative_ids[:, None] == entity_iota).astype(jnp.bfloat16)
    entity_grad = jnp.einsum(
        "se,sc->ec", asked_onehot, back_ent, preferred_element_type=jnp.float32
    ) + jnp.einsum(
        "se,sc->ec", neg_onehot, neg_grad.astype(jnp.bfloat16), preferred_element_type=jnp.float32
    )
    return (entity_grad.astype(jnp.bfloat16), relation_grad, loss)


def solution(mesh):
    return jax.shard_map(
        body,
        mesh=mesh,
        in_specs=(
            P(AXES, None),
            P(),
            P(AXES),
            P(AXES, None),
            P(AXES, None),
            P(AXES),
        ),
        out_specs=(P(AXES, None), P(), P(AXES)),
        check_vma=False,
    )
```

```python
import jax
import jax.numpy as jnp
from jax import lax
from jax.sharding import PartitionSpec as P

AXES = ("wide", "narrow")


def swap_halves(rows):
    half_width = rows.shape[-1] // 2
    return jnp.concatenate([rows[..., half_width:], rows[..., :half_width]], axis=-1)


def slot_ranks(targets):
    index = jnp.arange(targets.shape[0], dtype=jnp.int32)
    earlier_same = (targets[:, None] == targets[None, :]) & (index[:, None] < index[None, :])
    return jnp.sum(earlier_same.astype(jnp.int32), axis=0)


def body(entity_table, relation_table, triple_rel, triple_owners, triple_local, negative_ids):
    wide_count = lax.axis_size("wide")
    narrow_count = lax.axis_size("narrow")
    device_count = wide_count * narrow_count
    triples = triple_rel.shape[0]
    row_width = entity_table.shape[1]
    entity_rows = entity_table.shape[0]
    capacity = max(2, 4 * triples // device_count)
    rel_capacity = max(1, 2 * triples // device_count)
    rel_per_group = relation_table.shape[0] // device_count

    owners = jnp.concatenate([triple_owners[:, 0], triple_owners[:, 1]])
    local_rows = jnp.concatenate([triple_local[:, 0], triple_local[:, 1]])
    ent_pos = owners * capacity + slot_ranks(owners)
    rel_group = triple_rel // rel_per_group
    rel_pos = rel_group * rel_capacity + slot_ranks(rel_group)
    rel_local = triple_rel - rel_group * rel_per_group

    ent_place = jnp.arange(device_count * capacity, dtype=jnp.int32)[:, None] == ent_pos[None, :]
    rel_place = jnp.arange(device_count * rel_capacity, dtype=jnp.int32)[:, None] == rel_pos[None, :]
    send_ent_ids = jnp.sum(jnp.where(ent_place, local_rows[None, :], 0), axis=1)
    send_rel_ids = jnp.sum(jnp.where(rel_place, rel_local[None, :], 0), axis=1)
    send_ids = jnp.stack(
        [
            send_ent_ids.reshape(device_count, capacity),
            jnp.pad(
                send_rel_ids.reshape(device_count, rel_capacity), ((0, 0), (0, capacity - rel_capacity))
            ),
        ],
        axis=1,
    )
    recv_ids = lax.all_to_all(send_ids, AXES, split_axis=0, concat_axis=0, tiled=True)
    asked_ids = recv_ids[:, 0].reshape(-1)
    rel_ids_in = recv_ids[:, 1, :rel_capacity].reshape(-1)

    entity_iota = jnp.arange(entity_rows, dtype=jnp.int32)[None, :]
    asked_onehot = (asked_ids[:, None] == entity_iota).astype(jnp.bfloat16)
    served = jnp.einsum(
        "se,ec->sc", asked_onehot, entity_table, preferred_element_type=jnp.float32
    ).astype(jnp.bfloat16)
    served = served.reshape(device_count, capacity, row_width)
    got_rows = lax.all_to_all(served, AXES, split_axis=0, concat_axis=0, tiled=True)
    got_rows = got_rows.reshape(device_count * capacity, row_width)
    ent_place_bf = ent_place.astype(jnp.bfloat16)
    fetched = jnp.einsum(
        "sj,sc->jc", ent_place_bf, got_rows, preferred_element_type=jnp.float32
    ).astype(jnp.bfloat16)
    head_rows = fetched[:triples]
    tail_rows = fetched[triples:]
    rel_rows = jnp.take(relation_table, triple_rel, axis=0)
    query = (
        0.5 * swap_halves(head_rows).astype(jnp.float32) * swap_halves(rel_rows).astype(jnp.float32)
    ).astype(jnp.bfloat16)
    positive = jnp.sum(query.astype(jnp.float32) * tail_rows.astype(jnp.float32), axis=1)

    own_negs = jnp.take(entity_table, negative_ids, axis=0)
    gathered = lax.all_gather(own_negs, "narrow", axis=0, tiled=True)
    group_neg = gathered.shape[0]
    scores = jnp.einsum("tc,kc->tk", query, gathered, preferred_element_type=jnp.float32)
    neg_weights = (jax.nn.sigmoid(scores) / group_neg).astype(jnp.bfloat16)
    pos_weight = -jax.nn.sigmoid(-positive)
    query_grad = pos_weight[:, None] * tail_rows.astype(jnp.float32) + jnp.dot(
        neg_weights, gathered, preferred_element_type=jnp.float32
    )
    tail_grad = pos_weight[:, None] * query.astype(jnp.float32)
    head_grad = 0.5 * swap_halves(query_grad) * rel_rows.astype(jnp.float32)
    rel_part = 0.5 * swap_halves(query_grad) * head_rows.astype(jnp.float32)

    group_query = lax.all_gather(query, "narrow", axis=0, tiled=True)

    send_rel = jnp.einsum(
        "sj,jc->sc",
        rel_place.astype(jnp.bfloat16),
        rel_part.astype(jnp.bfloat16),
        preferred_element_type=jnp.float32,
    ).astype(jnp.bfloat16)
    send_rel, loss_scores, loss_positive = lax.optimization_barrier((send_rel, scores, positive))
    back_rel = lax.all_to_all(
        send_rel.reshape(device_count, rel_capacity, row_width), AXES, split_axis=0, concat_axis=0, tiled=True
    ).reshape(-1, row_width)
    loss = jax.nn.softplus(-loss_positive) + jnp.sum(jax.nn.softplus(loss_scores), axis=1) / group_neg
    rel_onehot = (
        rel_ids_in[:, None] == jnp.arange(rel_per_group, dtype=jnp.int32)[None, :]
    ).astype(jnp.bfloat16)
    own_rel_grad = jnp.einsum(
        "sr,sc->rc", rel_onehot, back_rel, preferred_element_type=jnp.float32
    ).astype(jnp.bfloat16)

    ent_grads = jnp.concatenate([head_grad, tail_grad], axis=0)
    send_ent = jnp.einsum(
        "sj,jc->sc", ent_place_bf, ent_grads.astype(jnp.bfloat16), preferred_element_type=jnp.float32
    ).astype(jnp.bfloat16)
    own_rel_grad, send_ent, group_query = lax.optimization_barrier((own_rel_grad, send_ent, group_query))
    relation_grad = lax.all_gather(own_rel_grad, AXES, axis=0, tiled=True)
    back_ent = lax.all_to_all(
        send_ent.reshape(device_count, capacity, row_width), AXES, split_axis=0, concat_axis=0, tiled=True
    ).reshape(-1, row_width)

    own_scores = jnp.einsum("tc,kc->tk", group_query, own_negs, preferred_element_type=jnp.float32)
    own_weights = (jax.nn.sigmoid(own_scores) / group_neg).astype(jnp.bfloat16)
    neg_grad = jnp.einsum("tk,tc->kc", own_weights, group_query, preferred_element_type=jnp.float32)

    neg_onehot = (negative_ids[:, None] == entity_iota).astype(jnp.bfloat16)
    entity_grad = jnp.einsum(
        "se,sc->ec", asked_onehot, back_ent, preferred_element_type=jnp.float32
    ) + jnp.einsum(
        "se,sc->ec", neg_onehot, neg_grad.astype(jnp.bfloat16), preferred_element_type=jnp.float32
    )
    return (entity_grad.astype(jnp.bfloat16), relation_grad, loss)


def solution(mesh):
    return jax.shard_map(
        body,
        mesh=mesh,
        in_specs=(
            P(AXES, None),
            P(),
            P(AXES),
            P(AXES, None),
            P(AXES, None),
            P(AXES),
        ),
        out_specs=(P(AXES, None), P(), P(AXES)),
        check_vma=False,
    )
```
